128 devices in a mesh: blk: 32 (over z, x_hi, y), rep: 4 (over x_lo, core).
Axes of the slice: x: 4 (x_hi: 2, x_lo: 2; x = x_hi * 2 + x_lo), y: 4, z: 4, core: 2. Of those that a mesh axis runs over, the one named last changes fastest.
Arguments:
- node_features: bfloat16 [49152, 512], P('blk', 'rep'), may hold values from -6 to 6
- weight: bfloat16 [512, 512], replicated, may hold values from -0.25 to 0.25
- cotangent: bfloat16 [49152, 512], P(('blk', 'rep')), may hold values from -6 to 6
- adjacency_tiles: bfloat16 [384, 56, 128, 128], P('blk'), as said below
- block_cols: int32 [384, 56], P('blk'), may hold values from 0 to 383, as said below
- block_perm: int32 [384], replicated, may hold values from 0 to 383, as said below
Outputs:
- activated: bfloat16 [49152, 512], P(('blk', 'rep'))
- feature_grad: bfloat16 [49152, 512], P('blk', 'rep')
- weight_grad: float32 [512, 512], P('rep')
The draws below stay inside these ranges and needn't reach their ends.
Inputs may be any that keep to these rules, and one draw needn't show every extreme that they name: Each row of block_cols names 56 different initial node blocks; if the row at position p (initial block q, block_perm[q] = p) names block c, then the row at position block_perm[c] names q. `block_perm`: each initial node block appears exactly once. `adjacency_tiles`: A is symmetric: the tile at row block p for column block c is the transpose of the tile at row block c for column block p.
All inputs are finite; a program needn't handle non-finite values.
Results may differ from the reference program's by a relative error of at most 0.0065.
Values may be sent and summed in bfloat16 or wider, within the bound.
No kernel may reach another device: no remote copies, remote signals or barrier semaphores. Data moves between devices by JAX's collectives and lax.ppermute only.
A program may use at most 128 MiB of HBM per device.

```python
import math
import jax
import jax.numpy as jnp
from jax import lax

F = 512
BS = 128
K_HALF = 28
K = 56
NBLK = 384
NODES = 49152


def pattern(key):
    perm_key = jax.random.fold_in(key, 11)
    offset_key = jax.random.fold_in(key, 12)
    block_perm = jax.random.permutation(perm_key, NBLK).astype(jnp.int32)
    offsets = (jax.random.permutation(offset_key, NBLK // 2 - 1)[:K_HALF] + 1).astype(jnp.int32)
    inverse = jnp.zeros((NBLK,), jnp.int32).at[block_perm].set(jnp.arange(NBLK, dtype=jnp.int32))
    return (block_perm, offsets, inverse)


def draw_block_perm(key, part):
    block_perm, offsets, inverse = pattern(key)
    return block_perm


def draw_block_cols(key, part):
    block_perm, offsets, inverse = pattern(key)
    initial = inverse[:, None]
    upper = (initial + offsets[None, :]) % NBLK
    lower = (initial - offsets[None, :]) % NBLK
    return jnp.concatenate([upper, lower], axis=1).astype(jnp.int32)


def draw_adjacency_tiles(key, part):
    block_perm, offsets, inverse = pattern(key)
    value_key = jax.random.fold_in(key, 13)
    values = jax.random.normal(value_key, (NBLK, K_HALF, BS, BS), jnp.float32)
    values = values * (1.0 / (BS * K) ** 0.5)
    forward = values[inverse]
    mirror_rows = (inverse[:, None] - offsets[None, :]) % NBLK
    slots = jnp.arange(K_HALF, dtype=jnp.int32)[None, :]
    mirrored = jnp.swapaxes(values[mirror_rows, slots], 2, 3)
    return jnp.concatenate([forward, mirrored], axis=1).astype(jnp.bfloat16)


def block_levels(rng, dims, split, smallest, top_value):
    level, own = 1.0, jax.random.fold_in(rng, 6)
    for dim, shards_of in split:
        steps = jnp.exp(jax.random.uniform(jax.random.fold_in(own, dim), (shards_of,), jnp.float32, smallest / len(split), top_value / len(split)))
        level = level * jnp.repeat(steps, dims[dim] // shards_of).reshape([-1 if axis == dim else 1 for axis in range(len(dims))])
    return level


def normal_values(key, dims, deviation, most, shards=(), kind=jnp.bfloat16):
    factor_of = block_levels(key, dims, shards, -0.22, 0.18) if shards else 1.0
    array = jax.random.normal(key, dims, jnp.float32) * deviation * factor_of
    return jnp.minimum(jnp.maximum(array, -most), most).astype(kind)


def setup_inputs(seed: int = 0) -> dict:
    streams_of = jax.random.split(jax.random.key(seed), 7)
    node_features = normal_values(streams_of[0], (NODES, F), 1.0, 6.0, ((0, 32), (1, 4)))
    weight = normal_values(streams_of[1], (F, F), F ** -0.5, 0.25)
    cotangent = normal_values(streams_of[2], (NODES, F), 1.0, 6.0, ((0, 128),))
    adjacency_tiles = draw_adjacency_tiles(jax.random.fold_in(streams_of[6], 71), 0)
    block_cols = draw_block_cols(jax.random.fold_in(streams_of[6], 71), 0)
    block_perm = draw_block_perm(jax.random.fold_in(streams_of[6], 71), 0)
    return dict(node_features=node_features, weight=weight, cotangent=cotangent, adjacency_tiles=adjacency_tiles, block_cols=block_cols, block_perm=block_perm)


def aggregate_with(adjacency_tiles, positions, field):
    blocks = field.reshape(NBLK, BS, F)

    def one_row(pieces):
        tile_row, source = pieces
        picked = jnp.take(blocks, source, axis=0).astype(jnp.float32)
        return jnp.einsum('kab,kbf->af', tile_row.astype(jnp.float32), picked)
    return lax.map(one_row, (adjacency_tiles, positions)).reshape(NODES, F)

def reference(node_features, weight, cotangent, adjacency_tiles, block_cols, block_perm):
    positions = jnp.take(block_perm, block_cols, axis=0).astype(jnp.int32)
    aggregate = aggregate_with(adjacency_tiles, positions, node_features).astype(jnp.bfloat16)
    preact = jnp.dot(aggregate, weight, preferred_element_type=jnp.float32)
    gating = jax.nn.sigmoid(preact)
    activated = (preact * gating).astype(jnp.bfloat16)
    slopes = gating * (1.0 + preact * (1.0 - gating))
    grad_pre = (cotangent.astype(jnp.float32) * slopes).astype(jnp.bfloat16)
    grad_agg = jnp.dot(grad_pre, weight.T, preferred_element_type=jnp.float32).astype(jnp.bfloat16)
    weight_grad = jnp.dot(aggregate.T, grad_pre, preferred_element_type=jnp.float32) * (1.0 / math.sqrt(NODES))
    feature_grad = aggregate_with(adjacency_tiles, positions, grad_agg).astype(jnp.bfloat16)
    return (activated, feature_grad, weight_grad)
```

```python
import math

import jax
import jax.numpy as jnp
from jax import lax
from jax.sharding import PartitionSpec as P


def column_positions(block_cols, block_perm):
    numbers = jnp.arange(block_perm.shape[0], dtype=jnp.int32)
    matches = block_cols[:, :, None] == numbers[None, None, :]
    return jnp.sum(jnp.where(matches, block_perm[None, None, :], 0), axis=-1)


def block_product(adjacency_tiles, positions, gathered):
    block_rows = adjacency_tiles.shape[2]
    blocks = gathered.reshape(-1, block_rows, gathered.shape[1])
    picked = blocks[positions]
    result = jnp.einsum(
        "pkab,pkbf->paf", adjacency_tiles, picked, preferred_element_type=jnp.float32
    )
    return result.reshape(-1, gathered.shape[1])


def xor_pairs(size, bit):
    return [(i, i ^ bit) for i in range(size)]


def butterfly_sum(x, axis):
    size = lax.axis_size(axis)
    bit = 1
    while bit < size:
        x = x + lax.ppermute(x, axis, xor_pairs(size, bit))
        bit *= 2
    return x


def halving_scatter(parts, axis):
    size = lax.axis_size(axis)
    me = lax.axis_index(axis)
    bit = size // 2
    while bit >= 1:
        half = parts.shape[0] // 2
        lo, hi = parts[:half], parts[half:]
        mine_hi = (me & bit) != 0
        keep = jnp.where(mine_hi, hi, lo)
        send = jnp.where(mine_hi, lo, hi)
        parts = keep + lax.ppermute(send, axis, xor_pairs(size, bit))
        bit //= 2
    return parts[0]


def local(node_features, weight, cotangent, adjacency_tiles, block_cols, block_perm):
    feat_dev = node_features.shape[1]
    n_rep = lax.axis_size("rep")
    f_all = weight.shape[0]
    w_split = weight.reshape(n_rep, feat_dev, f_all)
    positions = column_positions(block_cols, block_perm)
    gathered = lax.all_gather(node_features, "blk", axis=0, tiled=True)
    aggregate = block_product(adjacency_tiles, positions, gathered).astype(jnp.bfloat16)
    rows = aggregate.shape[0] // n_rep
    agg_rows = lax.all_to_all(aggregate, "rep", 0, 0, tiled=True).reshape(n_rep, rows, feat_dev)
    preact = jnp.einsum("irf,ifo->ro", agg_rows, w_split, preferred_element_type=jnp.float32)
    gating = jax.nn.sigmoid(preact)
    activated = (preact * gating).astype(jnp.bfloat16)
    slopes = gating * (1.0 + preact * (1.0 - gating))
    grad_pre = (cotangent.astype(jnp.float32) * slopes).astype(jnp.bfloat16)
    grad_split = jnp.einsum(
        "rf,jof->jro", grad_pre, w_split, preferred_element_type=jnp.float32
    ).astype(jnp.bfloat16)
    grad_agg = lax.all_to_all(grad_split.reshape(n_rep * rows, feat_dev), "rep", 0, 0, tiled=True)
    gathered_grad = lax.all_gather(grad_agg, "blk", axis=0, tiled=True)
    feature_grad = block_product(adjacency_tiles, positions, gathered_grad).astype(jnp.bfloat16)
    weight_part = jnp.einsum("irf,ro->ifo", agg_rows, grad_pre, preferred_element_type=jnp.float32)
    weight_rows = halving_scatter(weight_part, "rep")
    node_total = node_features.shape[0] * lax.axis_size("blk")
    weight_grad = butterfly_sum(weight_rows, "blk") * (1.0 / math.sqrt(node_total))
    return (activated, feature_grad, weight_grad)


def solution(mesh):
    return jax.shard_map(
        local,
        mesh=mesh,
        in_specs=(
            P("blk", "rep"),
            P(),
            P(("blk", "rep"), None),
            P("blk", None, None, None),
            P("blk", None),
            P(),
        ),
        out_specs=(P(("blk", "rep"), None), P("blk", "rep"), P("rep", None)),
        check_vma=False,
    )
```

```python
import math

import jax
import jax.numpy as jnp
from jax import lax
from jax.experimental import pallas as pl
from jax.experimental.pallas import tpu as pltpu
from jax.sharding import PartitionSpec as P


def column_positions(block_cols, block_perm):
    numbers = jnp.arange(block_perm.shape[0], dtype=jnp.int32)
    matches = block_cols[:, :, None] == numbers[None, None, :]
    return jnp.sum(jnp.where(matches, block_perm[None, None, :], 0), axis=-1)


def _product_kernel(pos_ref, a_ref, *refs):
    x_refs, o_ref = refs[:-1], refs[-1]
    acc = jnp.zeros(o_ref.shape[1:], jnp.float32)
    for k, x_ref in enumerate(x_refs):
        acc = acc + jnp.dot(a_ref[0, k], x_ref[0], preferred_element_type=jnp.float32)
    o_ref[0] = acc.astype(o_ref.dtype)


def block_product(adjacency_tiles, positions, gathered):
    rows, tiles, bs, _ = adjacency_tiles.shape
    width = gathered.shape[1]
    blocks = gathered.reshape(-1, bs, width)
    in_specs = [pl.BlockSpec((1, tiles, bs, bs), lambda p, pos: (p, 0, 0, 0))]
    for k in range(tiles):
        in_specs.append(
            pl.BlockSpec((1, bs, width), lambda p, pos, k=k: (pos[p * tiles + k], 0, 0))
        )
    cost = pl.CostEstimate(
        flops=2 * rows * tiles * bs * bs * width,
        bytes_accessed=2 * rows * tiles * bs * (bs + width) + 2 * rows * bs * width,
        transcendentals=0,
    )
    out = pl.pallas_call(
        _product_kernel,
        grid_spec=pltpu.PrefetchScalarGridSpec(
            num_scalar_prefetch=1,
            grid=(rows,),
            in_specs=in_specs,
            out_specs=pl.BlockSpec((1, bs, width), lambda p, pos: (p, 0, 0)),
        ),
        out_shape=jax.ShapeDtypeStruct((rows, bs, width), jnp.bfloat16),
        compiler_params=pltpu.CompilerParams(dimension_semantics=("arbitrary",)),
        cost_estimate=cost,
    )(positions.reshape(-1), adjacency_tiles, *([blocks] * tiles))
    return out.reshape(rows * bs, width)


def xor_pairs(size, bit):
    return [(i, i ^ bit) for i in range(size)]


def butterfly_sum(x, axis):
    size = lax.axis_size(axis)
    bit = 1
    while bit < size:
        x = x + lax.ppermute(x, axis, xor_pairs(size, bit))
        bit *= 2
    return x


def halving_scatter(parts, axis):
    size = lax.axis_size(axis)
    me = lax.axis_index(axis)
    bit = size // 2
    while bit >= 1:
        half = parts.shape[0] // 2
        lo, hi = parts[:half], parts[half:]
        mine_hi = (me & bit) != 0
        keep = jnp.where(mine_hi, hi, lo)
        send = jnp.where(mine_hi, lo, hi)
        parts = keep + lax.ppermute(send, axis, xor_pairs(size, bit))
        bit //= 2
    return parts[0]


def local(node_features, weight, cotangent, adjacency_tiles, block_cols, block_perm):
    feat_dev = node_features.shape[1]
    n_rep = lax.axis_size("rep")
    f_all = weight.shape[0]
    w_split = weight.reshape(n_rep, feat_dev, f_all)
    positions = column_positions(block_cols, block_perm)
    gathered = lax.all_gather(node_features, "blk", axis=0, tiled=True)
    aggregate = block_product(adjacency_tiles, positions, gathered)
    rows = aggregate.shape[0] // n_rep
    agg_rows = lax.all_to_all(aggregate, "rep", 0, 0, tiled=True).reshape(n_rep, rows, feat_dev)
    preact = jnp.einsum("irf,ifo->ro", agg_rows, w_split, preferred_element_type=jnp.float32)
    gating = jax.nn.sigmoid(preact)
    activated = (preact * gating).astype(jnp.bfloat16)
    slopes = gating * (1.0 + preact * (1.0 - gating))
    grad_pre = (cotangent.astype(jnp.float32) * slopes).astype(jnp.bfloat16)
    grad_split = jnp.einsum(
        "rf,jof->jro", grad_pre, w_split, preferred_element_type=jnp.float32
    ).astype(jnp.bfloat16)
    grad_agg = lax.all_to_all(grad_split.reshape(n_rep * rows, feat_dev), "rep", 0, 0, tiled=True)
    gathered_grad = lax.all_gather(grad_agg, "blk", axis=0, tiled=True)
    feature_grad = block_product(adjacency_tiles, positions, gathered_grad)
    weight_part = jnp.einsum("irf,ro->ifo", agg_rows, grad_pre, preferred_element_type=jnp.float32)
    weight_rows = halving_scatter(weight_part, "rep")
    node_total = node_features.shape[0] * lax.axis_size("blk")
    weight_grad = butterfly_sum(weight_rows, "blk") * (1.0 / math.sqrt(node_total))
    return (activated, feature_grad, weight_grad)


def solution(mesh):
    return jax.shard_map(
        local,
        mesh=mesh,
        in_specs=(
            P("blk", "rep"),
            P(),
            P(("blk", "rep"), None),
            P("blk", None, None, None),
            P("blk", None),
            P(),
        ),
        out_specs=(P(("blk", "rep"), None), P("blk", "rep"), P("rep", None)),
        check_vma=False,
    )
```

```python
import functools
import math

import jax
import jax.numpy as jnp
from jax import lax
from jax.experimental import pallas as pl
from jax.experimental.pallas import tpu as pltpu
from jax.sharding import Mesh, PartitionSpec as P


def column_positions(block_cols, block_perm):
    numbers = jnp.arange(block_perm.shape[0], dtype=jnp.int32)
    matches = block_cols[:, :, None] == numbers[None, None, :]
    return jnp.sum(jnp.where(matches, block_perm[None, None, :], 0), axis=-1)


def _product_kernel(pos_ref, a_ref, *refs):
    x_refs, o_ref = refs[:-1], refs[-1]
    acc = jnp.zeros(o_ref.shape[1:], jnp.float32)
    for k, x_ref in enumerate(x_refs):
        acc = acc + jnp.dot(a_ref[0, k], x_ref[0], preferred_element_type=jnp.float32)
    o_ref[0] = acc.astype(o_ref.dtype)


def block_product(adjacency_tiles, positions, gathered):
    rows, tiles, bs, _ = adjacency_tiles.shape
    width = gathered.shape[1]
    blocks = gathered.reshape(-1, bs, width)
    in_specs = [pl.BlockSpec((1, tiles, bs, bs), lambda p, pos: (p, 0, 0, 0))]
    for k in range(tiles):
        in_specs.append(
            pl.BlockSpec((1, bs, width), lambda p, pos, k=k: (pos[p * tiles + k], 0, 0))
        )
    cost = pl.CostEstimate(
        flops=2 * rows * tiles * bs * bs * width,
        bytes_accessed=2 * rows * tiles * bs * (bs + width) + 2 * rows * bs * width,
        transcendentals=0,
    )
    out = pl.pallas_call(
        _product_kernel,
        grid_spec=pltpu.PrefetchScalarGridSpec(
            num_scalar_prefetch=1,
            grid=(rows,),
            in_specs=in_specs,
            out_specs=pl.BlockSpec((1, bs, width), lambda p, pos: (p, 0, 0)),
        ),
        out_shape=jax.ShapeDtypeStruct((rows, bs, width), jnp.bfloat16),
        compiler_params=pltpu.CompilerParams(dimension_semantics=("arbitrary",)),
        cost_estimate=cost,
    )(positions.reshape(-1), adjacency_tiles, *([blocks] * tiles))
    return out.reshape(rows * bs, width)


def xor_pairs(size, bit):
    return [(i, i ^ bit) for i in range(size)]


def butterfly_sum(x, axis, size):
    bit = 1
    while bit < size:
        x = x + lax.ppermute(x, axis, xor_pairs(size, bit))
        bit *= 2
    return x


def halving_scatter(parts, axis, size):
    me = lax.axis_index(axis)
    bit = size // 2
    while bit >= 1:
        half = parts.shape[0] // 2
        lo, hi = parts[:half], parts[half:]
        mine_hi = (me & bit) != 0
        keep = jnp.where(mine_hi, hi, lo)
        send = jnp.where(mine_hi, lo, hi)
        parts = keep + lax.ppermute(send, axis, xor_pairs(size, bit))
        bit //= 2
    return parts[0]


BLK = ("z", "xh", "y")
REP = ("xl", "c")


def hier_gather(x):
    pair = lax.all_gather(x, "xh", axis=0, tiled=True)
    return lax.all_gather(pair, ("z", "y"), axis=0, tiled=True)


def hier_positions(positions, local_blocks, n_xh, n_y):
    owner, block = positions // local_blocks, positions % local_blocks
    z, xh, y = owner // (n_xh * n_y), (owner // n_y) % n_xh, owner % n_y
    return ((z * n_y + y) * n_xh + xh) * local_blocks + block


def local(sizes, node_features, weight, cotangent, adjacency_tiles, block_cols, block_perm):
    n_z, n_xh, n_y, n_xl, n_c = sizes
    n_blk, n_rep = n_z * n_xh * n_y, n_xl * n_c
    feat_dev = node_features.shape[1]
    f_all = weight.shape[0]
    bs = adjacency_tiles.shape[2]
    w_split = weight.reshape(n_rep, feat_dev, f_all)
    positions = column_positions(block_cols, block_perm)
    positions = hier_positions(positions, node_features.shape[0] // bs, n_xh, n_y)
    gathered = hier_gather(node_features)
    aggregate = block_product(adjacency_tiles, positions, gathered)
    rows = aggregate.shape[0] // n_rep
    agg_rows = lax.all_to_all(aggregate, REP, 0, 0, tiled=True).reshape(n_rep, rows, feat_dev)
    preact = jnp.einsum("irf,ifo->ro", agg_rows, w_split, preferred_element_type=jnp.float32)
    gating = jax.nn.sigmoid(preact)
    activated = (preact * gating).astype(jnp.bfloat16)
    slopes = gating * (1.0 + preact * (1.0 - gating))
    grad_pre = (cotangent.astype(jnp.float32) * slopes).astype(jnp.bfloat16)
    grad_split = jnp.einsum(
        "rf,jof->jro", grad_pre, w_split, preferred_element_type=jnp.float32
    ).astype(jnp.bfloat16)
    grad_agg = lax.all_to_all(grad_split.reshape(n_rep * rows, feat_dev), REP, 0, 0, tiled=True)
    gathered_grad = hier_gather(grad_agg)
    feature_grad = block_product(adjacency_tiles, positions, gathered_grad)
    weight_part = jnp.einsum("irf,ro->ifo", agg_rows, grad_pre, preferred_element_type=jnp.float32)
    weight_rows = halving_scatter(weight_part, REP, n_rep)
    node_total = node_features.shape[0] * n_blk
    weight_grad = butterfly_sum(weight_rows, BLK, n_blk) * (1.0 / math.sqrt(node_total))
    return (activated, feature_grad, weight_grad)


def solution(mesh):
    n_blk, n_rep = mesh.shape["blk"], mesh.shape["rep"]
    sizes = (n_blk // 8, 2, 4, n_rep // 2, 2)
    fine = Mesh(mesh.devices.reshape(sizes), BLK + REP)
    return jax.shard_map(
        functools.partial(local, sizes),
        mesh=fine,
        in_specs=(
            P(BLK, REP),
            P(),
            P(BLK + REP, None),
            P(BLK, None, None, None),
            P(BLK, None),
            P(),
        ),
        out_specs=(P(BLK + REP, None), P(BLK, REP), P(REP, None)),
        check_vma=False,
    )
```

```python
import functools
import math

import jax
import jax.numpy as jnp
from jax import lax
from jax.experimental import pallas as pl
from jax.experimental.pallas import tpu as pltpu
from jax.sharding import Mesh, PartitionSpec as P


def column_positions(block_cols, block_perm):
    numbers = jnp.arange(block_perm.shape[0], dtype=jnp.int32)
    matches = block_cols[:, :, None] == numbers[None, None, :]
    return jnp.sum(jnp.where(matches, block_perm[None, None, :], 0), axis=-1)


def _product_kernel(pos_ref, a_ref, *refs):
    x_refs, o_ref = refs[:-1], refs[-1]
    acc = jnp.zeros(o_ref.shape[1:], jnp.float32)
    for k, x_ref in enumerate(x_refs):
        acc = acc + jnp.dot(a_ref[0, k], x_ref[0], preferred_element_type=jnp.float32)
    o_ref[0] = acc.astype(o_ref.dtype)


def block_product(adjacency_tiles, positions, gathered):
    rows, tiles, bs, _ = adjacency_tiles.shape
    width = gathered.shape[1]
    blocks = gathered.reshape(-1, bs, width)
    in_specs = [pl.BlockSpec((1, tiles, bs, bs), lambda p, pos: (p, 0, 0, 0))]
    for k in range(tiles):
        in_specs.append(
            pl.BlockSpec((1, bs, width), lambda p, pos, k=k: (pos[p * tiles + k], 0, 0))
        )
    cost = pl.CostEstimate(
        flops=2 * rows * tiles * bs * bs * width,
        bytes_accessed=2 * rows * tiles * bs * (bs + width) + 2 * rows * bs * width,
        transcendentals=0,
    )
    out = pl.pallas_call(
        _product_kernel,
        grid_spec=pltpu.PrefetchScalarGridSpec(
            num_scalar_prefetch=1,
            grid=(rows,),
            in_specs=in_specs,
            out_specs=pl.BlockSpec((1, bs, width), lambda p, pos: (p, 0, 0)),
        ),
        out_shape=jax.ShapeDtypeStruct((rows, bs, width), jnp.bfloat16),
        compiler_params=pltpu.CompilerParams(dimension_semantics=("arbitrary",)),
        cost_estimate=cost,
    )(positions.reshape(-1), adjacency_tiles, *([blocks] * tiles))
    return out.reshape(rows * bs, width)


def xor_pairs(size, bit):
    return [(i, i ^ bit) for i in range(size)]


def butterfly_sum(x, axis, size):
    bit = 1
    while bit < size:
        x = x + lax.ppermute(x, axis, xor_pairs(size, bit))
        bit *= 2
    return x


def halving_scatter(parts, axis, size):
    me = lax.axis_index(axis)
    bit = size // 2
    while bit >= 1:
        half = parts.shape[0] // 2
        lo, hi = parts[:half], parts[half:]
        mine_hi = (me & bit) != 0
        keep = jnp.where(mine_hi, hi, lo)
        send = jnp.where(mine_hi, lo, hi)
        parts = keep + lax.ppermute(send, axis, xor_pairs(size, bit))
        bit //= 2
    return parts[0]


BLK = ("z", "xh", "y")
REP = ("xl", "c")


def exchange(parts, axis, size):
    me = lax.axis_index(axis)
    got = [lax.dynamic_index_in_dim(parts, me, 0, keepdims=False)]
    for s in range(1, size):
        send = lax.dynamic_index_in_dim(parts, me ^ s, 0, keepdims=False)
        got.append(lax.ppermute(send, axis, xor_pairs(size, s)))
    return jnp.take(jnp.stack(got), jnp.arange(size) ^ me, axis=0)


def hier_gather(x):
    partner = lax.ppermute(x, "xh", xor_pairs(2, 1))
    pair = jnp.concatenate([x, partner], axis=0)
    return lax.all_gather(pair, ("z", "y"), axis=0, tiled=True)


def hier_positions(positions, local_blocks, n_xh, n_y):
    owner, block = positions // local_blocks, positions % local_blocks
    z, xh, y = owner // (n_xh * n_y), (owner // n_y) % n_xh, owner % n_y
    slot = xh ^ lax.axis_index("xh")
    return ((z * n_y + y) * n_xh + slot) * local_blocks + block


def local(sizes, node_features, weight, cotangent, adjacency_tiles, block_cols, block_perm):
    n_z, n_xh, n_y, n_xl, n_c = sizes
    n_blk, n_rep = n_z * n_xh * n_y, n_xl * n_c
    feat_dev = node_features.shape[1]
    f_all = weight.shape[0]
    bs = adjacency_tiles.shape[2]
    w_split = weight.reshape(n_rep, feat_dev, f_all)
    positions = column_positions(block_cols, block_perm)
    positions = hier_positions(positions, node_features.shape[0] // bs, n_xh, n_y)
    gathered = hier_gather(node_features)
    aggregate = block_product(adjacency_tiles, positions, gathered)
    rows = aggregate.shape[0] // n_rep
    agg_rows = exchange(aggregate.reshape(n_rep, rows, feat_dev), REP, n_rep)
    preact = jnp.einsum("irf,ifo->ro", agg_rows, w_split, preferred_element_type=jnp.float32)
    gating = jax.nn.sigmoid(preact)
    activated = (preact * gating).astype(jnp.bfloat16)
    slopes = gating * (1.0 + preact * (1.0 - gating))
    grad_pre = (cotangent.astype(jnp.float32) * slopes).astype(jnp.bfloat16)
    grad_split = jnp.einsum(
        "rf,jof->jro", grad_pre, w_split, preferred_element_type=jnp.float32
    ).astype(jnp.bfloat16)
    grad_agg = exchange(grad_split, REP, n_rep).reshape(n_rep * rows, feat_dev)
    gathered_grad = hier_gather(grad_agg)
    feature_grad = block_product(adjacency_tiles, positions, gathered_grad)
    weight_part = jnp.einsum("irf,ro->ifo", agg_rows, grad_pre, preferred_element_type=jnp.float32)
    weight_rows = halving_scatter(weight_part, REP, n_rep)
    node_total = node_features.shape[0] * n_blk
    weight_grad = butterfly_sum(weight_rows, BLK, n_blk) * (1.0 / math.sqrt(node_total))
    return (activated, feature_grad, weight_grad)


def solution(mesh):
    n_blk, n_rep = mesh.shape["blk"], mesh.shape["rep"]
    sizes = (n_blk // 8, 2, 4, n_rep // 2, 2)
    fine = Mesh(mesh.devices.reshape(sizes), BLK + REP)
    return jax.shard_map(
        functools.partial(local, sizes),
        mesh=fine,
        in_specs=(
            P(BLK, REP),
            P(),
            P(BLK + REP, None),
            P(BLK, None, None, None),
            P(BLK, None),
            P(),
        ),
        out_specs=(P(BLK + REP, None), P(BLK, REP), P(REP, None)),
        check_vma=False,
    )
```

```python
import functools
import math

import jax
import jax.numpy as jnp
from jax import lax
from jax.experimental import pallas as pl
from jax.experimental.pallas import tpu as pltpu
from jax.sharding import Mesh, PartitionSpec as P


def column_positions(block_cols, block_perm):
    numbers = jnp.arange(block_perm.shape[0], dtype=jnp.int32)
    matches = block_cols[:, :, None] == numbers[None, None, :]
    return jnp.sum(jnp.where(matches, block_perm[None, None, :], 0), axis=-1)


def _product_kernel(has_init, pos_ref, use_ref, a_ref, *refs):
    if has_init:
        init_ref, refs = refs[0], refs[1:]
    x_refs, o_ref, acc_ref = refs[:-2], refs[-2], refs[-1]
    p = pl.program_id(0)
    tiles = len(x_refs)
    if has_init:
        acc_ref[...] = init_ref[0]
    else:
        acc_ref[...] = jnp.zeros(acc_ref.shape, jnp.float32)
    for k, x_ref in enumerate(x_refs):

        @pl.when(use_ref[p * tiles + k] != 0)
        def _():
            acc_ref[...] += jnp.dot(a_ref[0, k], x_ref[0], preferred_element_type=jnp.float32)

    o_ref[0] = acc_ref[...].astype(o_ref.dtype)


def block_product(adjacency_tiles, index, use, gathered, init, out_dtype):
    rows, tiles, bs, _ = adjacency_tiles.shape
    width = gathered.shape[1]
    blocks = gathered.reshape(-1, bs, width)
    has_init = init is not None
    in_specs = [pl.BlockSpec((1, tiles, bs, bs), lambda p, pos, use: (p, 0, 0, 0))]
    operands = [adjacency_tiles]
    if has_init:
        in_specs.append(pl.BlockSpec((1, bs, width), lambda p, pos, use: (p, 0, 0)))
        operands.append(init)
    for k in range(tiles):
        in_specs.append(
            pl.BlockSpec((1, bs, width), lambda p, pos, use, k=k: (pos[p * tiles + k], 0, 0))
        )
    operands += [blocks] * tiles
    cost = pl.CostEstimate(
        flops=rows * tiles * bs * bs * width,
        bytes_accessed=2 * rows * tiles * bs * bs + rows * tiles * bs * width + 6 * rows * bs * width,
        transcendentals=0,
    )
    out = pl.pallas_call(
        functools.partial(_product_kernel, has_init),
        grid_spec=pltpu.PrefetchScalarGridSpec(
            num_scalar_prefetch=2,
            grid=(rows,),
            in_specs=in_specs,
            out_specs=pl.BlockSpec((1, bs, width), lambda p, pos, use: (p, 0, 0)),
            scratch_shapes=[pltpu.VMEM((bs, width), jnp.float32)],
        ),
        out_shape=jax.ShapeDtypeStruct((rows, bs, width), out_dtype),
        compiler_params=pltpu.CompilerParams(dimension_semantics=("arbitrary",)),
        cost_estimate=cost,
    )(index.reshape(-1), use.reshape(-1), *operands)
    return out


def split_product(adjacency_tiles, plan, near, far):
    near_index, near_use, far_index, far_use = plan
    partial = block_product(adjacency_tiles, near_index, near_use, near, None, jnp.float32)
    out = block_product(adjacency_tiles, far_index, far_use, far, partial, jnp.bfloat16)
    return out.reshape(-1, near.shape[1])


def xor_pairs(size, bit):
    return [(i, i ^ bit) for i in range(size)]


def butterfly_sum(x, axis, size):
    bit = 1
    while bit < size:
        x = x + lax.ppermute(x, axis, xor_pairs(size, bit))
        bit *= 2
    return x


def halving_scatter(parts, axis, size):
    me = lax.axis_index(axis)
    bit = size // 2
    while bit >= 1:
        half = parts.shape[0] // 2
        lo, hi = parts[:half], parts[half:]
        mine_hi = (me & bit) != 0
        keep = jnp.where(mine_hi, hi, lo)
        send = jnp.where(mine_hi, lo, hi)
        parts = keep + lax.ppermute(send, axis, xor_pairs(size, bit))
        bit //= 2
    return parts[0]


BLK = ("z", "xh", "y")
REP = ("xl", "c")


def exchange(parts, axis, size):
    me = lax.axis_index(axis)
    got = [lax.dynamic_index_in_dim(parts, me, 0, keepdims=False)]
    for s in range(1, size):
        send = lax.dynamic_index_in_dim(parts, me ^ s, 0, keepdims=False)
        got.append(lax.ppermute(send, axis, xor_pairs(size, s)))
    return jnp.take(jnp.stack(got), jnp.arange(size) ^ me, axis=0)


def split_gather(x):
    near = lax.all_gather(x, ("z", "y"), axis=0, tiled=True)
    partner = lax.ppermute(x, "xh", xor_pairs(2, 1))
    far = lax.all_gather(partner, ("z", "y"), axis=0, tiled=True)
    return near, far


def split_plan(positions, local_blocks, n_xh, n_y):
    owner, block = positions // local_blocks, positions % local_blocks
    z, xh, y = owner // (n_xh * n_y), (owner // n_y) % n_xh, owner % n_y
    index = (z * n_y + y) * local_blocks + block
    near = xh == lax.axis_index("xh")
    zero = jnp.zeros_like(index)
    return (
        jnp.where(near, index, zero),
        near.astype(jnp.int32),
        jnp.where(near, zero, index),
        (~near).astype(jnp.int32),
    )


def local(sizes, node_features, weight, cotangent, adjacency_tiles, block_cols, block_perm):
    n_z, n_xh, n_y, n_xl, n_c = sizes
    n_blk, n_rep = n_z * n_xh * n_y, n_xl * n_c
    feat_dev = node_features.shape[1]
    f_all = weight.shape[0]
    bs = adjacency_tiles.shape[2]
    w_split = weight.reshape(n_rep, feat_dev, f_all)
    positions = column_positions(block_cols, block_perm)
    plan = split_plan(positions, node_features.shape[0] // bs, n_xh, n_y)
    aggregate = split_product(adjacency_tiles, plan, *split_gather(node_features))
    rows = aggregate.shape[0] // n_rep
    agg_rows = exchange(aggregate.reshape(n_rep, rows, feat_dev), REP, n_rep)
    preact = jnp.einsum("irf,ifo->ro", agg_rows, w_split, preferred_element_type=jnp.float32)
    gating = jax.nn.sigmoid(preact)
    activated = (preact * gating).astype(jnp.bfloat16)
    slopes = gating * (1.0 + preact * (1.0 - gating))
    grad_pre = (cotangent.astype(jnp.float32) * slopes).astype(jnp.bfloat16)
    grad_split = jnp.einsum(
        "rf,jof->jro", grad_pre, w_split, preferred_element_type=jnp.float32
    ).astype(jnp.bfloat16)
    grad_agg = exchange(grad_split, REP, n_rep).reshape(n_rep * rows, feat_dev)
    feature_grad = split_product(adjacency_tiles, plan, *split_gather(grad_agg))
    weight_part = jnp.einsum("irf,ro->ifo", agg_rows, grad_pre, preferred_element_type=jnp.float32)
    weight_rows = halving_scatter(weight_part, REP, n_rep)
    node_total = node_features.shape[0] * n_blk
    weight_grad = butterfly_sum(weight_rows, BLK, n_blk) * (1.0 / math.sqrt(node_total))
    return (activated, feature_grad, weight_grad)


def solution(mesh):
    n_blk, n_rep = mesh.shape["blk"], mesh.shape["rep"]
    sizes = (n_blk // 8, 2, 4, n_rep // 2, 2)
    fine = Mesh(mesh.devices.reshape(sizes), BLK + REP)
    return jax.shard_map(
        functools.partial(local, sizes),
        mesh=fine,
        in_specs=(
            P(BLK, REP),
            P(),
            P(BLK + REP, None),
            P(BLK, None, None, None),
            P(BLK, None),
            P(),
        ),
        out_specs=(P(BLK + REP, None), P(BLK, REP), P(REP, None)),
        check_vma=False,
    )
```

```python
import functools
import math

import jax
import jax.numpy as jnp
from jax import lax
from jax.experimental import pallas as pl
from jax.experimental.pallas import tpu as pltpu
from jax.sharding import Mesh, PartitionSpec as P


def column_positions(block_cols, block_perm):
    numbers = jnp.arange(block_perm.shape[0], dtype=jnp.int32)
    matches = block_cols[:, :, None] == numbers[None, None, :]
    return jnp.sum(jnp.where(matches, block_perm[None, None, :], 0), axis=-1)


def _product_kernel(pos_ref, a_ref, *refs):
    x_refs, o_ref = refs[:-1], refs[-1]
    lhs = jnp.concatenate([a_ref[0, k] for k in range(len(x_refs))], axis=1)
    rhs = jnp.concatenate([x_ref[0] for x_ref in x_refs], axis=0)
    o_ref[0] = jnp.dot(lhs, rhs, preferred_element_type=jnp.float32).astype(o_ref.dtype)


def block_product(adjacency_tiles, positions, gathered):
    rows, tiles, bs, _ = adjacency_tiles.shape
    width = gathered.shape[1]
    blocks = gathered.reshape(-1, bs, width)
    in_specs = [pl.BlockSpec((1, tiles, bs, bs), lambda p, pos: (p, 0, 0, 0))]
    for k in range(tiles):
        in_specs.append(
            pl.BlockSpec((1, bs, width), lambda p, pos, k=k: (pos[p * tiles + k], 0, 0))
        )
    cost = pl.CostEstimate(
        flops=2 * rows * tiles * bs * bs * width,
        bytes_accessed=2 * rows * tiles * bs * (bs + width) + 2 * rows * bs * width,
        transcendentals=0,
    )
    out = pl.pallas_call(
        _product_kernel,
        grid_spec=pltpu.PrefetchScalarGridSpec(
            num_scalar_prefetch=1,
            grid=(rows,),
            in_specs=in_specs,
            out_specs=pl.BlockSpec((1, bs, width), lambda p, pos: (p, 0, 0)),
        ),
        out_shape=jax.ShapeDtypeStruct((rows, bs, width), jnp.bfloat16),
        compiler_params=pltpu.CompilerParams(dimension_semantics=("arbitrary",)),
        cost_estimate=cost,
    )(positions.reshape(-1), adjacency_tiles, *([blocks] * tiles))
    return out.reshape(rows * bs, width)


def xor_pairs(size, bit):
    return [(i, i ^ bit) for i in range(size)]


def butterfly_sum(x, axis, size):
    bit = 1
    while bit < size:
        x = x + lax.ppermute(x, axis, xor_pairs(size, bit))
        bit *= 2
    return x


def halving_scatter(parts, axis, size):
    me = lax.axis_index(axis)
    bit = size // 2
    while bit >= 1:
        half = parts.shape[0] // 2
        lo, hi = parts[:half], parts[half:]
        mine_hi = (me & bit) != 0
        keep = jnp.where(mine_hi, hi, lo)
        send = jnp.where(mine_hi, lo, hi)
        parts = keep + lax.ppermute(send, axis, xor_pairs(size, bit))
        bit //= 2
    return parts[0]


BLK = ("z", "xh", "y")
REP = ("xl", "c")


def exchange(parts, axis, size):
    me = lax.axis_index(axis)
    got = [lax.dynamic_index_in_dim(parts, me, 0, keepdims=False)]
    for s in range(1, size):
        send = lax.dynamic_index_in_dim(parts, me ^ s, 0, keepdims=False)
        got.append(lax.ppermute(send, axis, xor_pairs(size, s)))
    return jnp.take(jnp.stack(got), jnp.arange(size) ^ me, axis=0)


def hier_gather(x):
    partner = lax.ppermute(x, "xh", xor_pairs(2, 1))
    pair = jnp.concatenate([x, partner], axis=0)
    return lax.all_gather(pair, ("z", "y"), axis=0, tiled=True)


def hier_positions(positions, local_blocks, n_xh, n_y):
    owner, block = positions // local_blocks, positions % local_blocks
    z, xh, y = owner // (n_xh * n_y), (owner // n_y) % n_xh, owner % n_y
    slot = xh ^ lax.axis_index("xh")
    return ((z * n_y + y) * n_xh + slot) * local_blocks + block


def local(sizes, node_features, weight, cotangent, adjacency_tiles, block_cols, block_perm):
    n_z, n_xh, n_y, n_xl, n_c = sizes
    n_blk, n_rep = n_z * n_xh * n_y, n_xl * n_c
    feat_dev = node_features.shape[1]
    f_all = weight.shape[0]
    bs = adjacency_tiles.shape[2]
    w_split = weight.reshape(n_rep, feat_dev, f_all)
    positions = column_positions(block_cols, block_perm)
    positions = hier_positions(positions, node_features.shape[0] // bs, n_xh, n_y)
    gathered = hier_gather(node_features)
    aggregate = block_product(adjacency_tiles, positions, gathered)
    rows = aggregate.shape[0] // n_rep
    agg_rows = exchange(aggregate.reshape(n_rep, rows, feat_dev), REP, n_rep)
    preact = jnp.einsum("irf,ifo->ro", agg_rows, w_split, preferred_element_type=jnp.float32)
    gating = jax.nn.sigmoid(preact)
    activated = (preact * gating).astype(jnp.bfloat16)
    slopes = gating * (1.0 + preact * (1.0 - gating))
    grad_pre = (cotangent.astype(jnp.float32) * slopes).astype(jnp.bfloat16)
    grad_split = jnp.einsum(
        "rf,jof->jro", grad_pre, w_split, preferred_element_type=jnp.float32
    ).astype(jnp.bfloat16)
    grad_agg = exchange(grad_split, REP, n_rep).reshape(n_rep * rows, feat_dev)
    gathered_grad = hier_gather(grad_agg)
    feature_grad = block_product(adjacency_tiles, positions, gathered_grad)
    weight_part = jnp.einsum("irf,ro->ifo", agg_rows, grad_pre, preferred_element_type=jnp.float32)
    weight_rows = halving_scatter(weight_part, REP, n_rep)
    node_total = node_features.shape[0] * n_blk
    weight_grad = butterfly_sum(weight_rows, BLK, n_blk) * (1.0 / math.sqrt(node_total))
    return (activated, feature_grad, weight_grad)


def solution(mesh):
    n_blk, n_rep = mesh.shape["blk"], mesh.shape["rep"]
    sizes = (n_blk // 8, 2, 4, n_rep // 2, 2)
    fine = Mesh(mesh.devices.reshape(sizes), BLK + REP)
    return jax.shard_map(
        functools.partial(local, sizes),
        mesh=fine,
        in_specs=(
            P(BLK, REP),
            P(),
            P(BLK + REP, None),
            P(BLK, None, None, None),
            P(BLK, None),
            P(),
        ),
        out_specs=(P(BLK + REP, None), P(BLK, REP), P(REP, None)),
        check_vma=False,
    )
```

```python
import functools
import math

import jax
import jax.numpy as jnp
from jax import lax
from jax.experimental import pallas as pl
from jax.experimental.pallas import tpu as pltpu
from jax.sharding import Mesh, PartitionSpec as P


def column_positions(block_cols, block_perm):
    numbers = jnp.arange(block_perm.shape[0], dtype=jnp.int32)
    matches = block_cols[:, :, None] == numbers[None, None, :]
    return jnp.sum(jnp.where(matches, block_perm[None, None, :], 0), axis=-1)


def _product_kernel(pos_ref, a_ref, x_ref, o_ref):
    p = pl.program_id(0)
    tiles = a_ref.shape[1]
    lhs = jnp.concatenate([a_ref[0, k] for k in range(tiles)], axis=1)
    rhs = jnp.concatenate([x_ref[pos_ref[p * tiles + k]] for k in range(tiles)], axis=0)
    o_ref[0] = jnp.dot(lhs, rhs, preferred_element_type=jnp.float32).astype(o_ref.dtype)


def block_product(adjacency_tiles, positions, gathered):
    rows, tiles, bs, _ = adjacency_tiles.shape
    width = gathered.shape[1]
    blocks = gathered.reshape(-1, bs, width)
    cost = pl.CostEstimate(
        flops=2 * rows * tiles * bs * bs * width,
        bytes_accessed=2 * rows * tiles * bs * bs + 2 * blocks.size + 2 * rows * bs * width,
        transcendentals=0,
    )
    out = pl.pallas_call(
        _product_kernel,
        grid_spec=pltpu.PrefetchScalarGridSpec(
            num_scalar_prefetch=1,
            grid=(rows,),
            in_specs=[
                pl.BlockSpec((1, tiles, bs, bs), lambda p, pos: (p, 0, 0, 0)),
                pl.BlockSpec(blocks.shape, lambda p, pos: (0, 0, 0), pipeline_mode=pl.Buffered(1)),
            ],
            out_specs=pl.BlockSpec((1, bs, width), lambda p, pos: (p, 0, 0)),
        ),
        out_shape=jax.ShapeDtypeStruct((rows, bs, width), jnp.bfloat16),
        compiler_params=pltpu.CompilerParams(
            dimension_semantics=("arbitrary",), vmem_limit_bytes=48 * 1024 * 1024
        ),
        cost_estimate=cost,
    )(positions.reshape(-1), adjacency_tiles, blocks)
    return out.reshape(rows * bs, width)


def xor_pairs(size, bit):
    return [(i, i ^ bit) for i in range(size)]


def butterfly_sum(x, axis, size):
    bit = 1
    while bit < size:
        x = x + lax.ppermute(x, axis, xor_pairs(size, bit))
        bit *= 2
    return x


def halving_scatter(parts, axis, size):
    me = lax.axis_index(axis)
    bit = size // 2
    while bit >= 1:
        half = parts.shape[0] // 2
        lo, hi = parts[:half], parts[half:]
        mine_hi = (me & bit) != 0
        keep = jnp.where(mine_hi, hi, lo)
        send = jnp.where(mine_hi, lo, hi)
        parts = keep + lax.ppermute(send, axis, xor_pairs(size, bit))
        bit //= 2
    return parts[0]


BLK = ("z", "xh", "y")
REP = ("xl", "c")


def exchange(parts, axis, size):
    me = lax.axis_index(axis)
    got = [lax.dynamic_index_in_dim(parts, me, 0, keepdims=False)]
    for s in range(1, size):
        send = lax.dynamic_index_in_dim(parts, me ^ s, 0, keepdims=False)
        got.append(lax.ppermute(send, axis, xor_pairs(size, s)))
    return jnp.take(jnp.stack(got), jnp.arange(size) ^ me, axis=0)


def hier_gather(x):
    partner = lax.ppermute(x, "xh", xor_pairs(2, 1))
    pair = jnp.concatenate([x, partner], axis=0)
    return lax.all_gather(pair, ("z", "y"), axis=0, tiled=True)


def hier_positions(positions, local_blocks, n_xh, n_y):
    owner, block = positions // local_blocks, positions % local_blocks
    z, xh, y = owner // (n_xh * n_y), (owner // n_y) % n_xh, owner % n_y
    slot = xh ^ lax.axis_index("xh")
    return ((z * n_y + y) * n_xh + slot) * local_blocks + block


def local(sizes, node_features, weight, cotangent, adjacency_tiles, block_cols, block_perm):
    n_z, n_xh, n_y, n_xl, n_c = sizes
    n_blk, n_rep = n_z * n_xh * n_y, n_xl * n_c
    feat_dev = node_features.shape[1]
    f_all = weight.shape[0]
    bs = adjacency_tiles.shape[2]
    w_split = weight.reshape(n_rep, feat_dev, f_all)
    positions = column_positions(block_cols, block_perm)
    positions = hier_positions(positions, node_features.shape[0] // bs, n_xh, n_y)
    gathered = hier_gather(node_features)
    aggregate = block_product(adjacency_tiles, positions, gathered)
    rows = aggregate.shape[0] // n_rep
    agg_rows = exchange(aggregate.reshape(n_rep, rows, feat_dev), REP, n_rep)
    preact = jnp.einsum("irf,ifo->ro", agg_rows, w_split, preferred_element_type=jnp.float32)
    gating = jax.nn.sigmoid(preact)
    activated = (preact * gating).astype(jnp.bfloat16)
    slopes = gating * (1.0 + preact * (1.0 - gating))
    grad_pre = (cotangent.astype(jnp.float32) * slopes).astype(jnp.bfloat16)
    grad_split = jnp.einsum(
        "rf,jof->jro", grad_pre, w_split, preferred_element_type=jnp.float32
    ).astype(jnp.bfloat16)
    grad_agg = exchange(grad_split, REP, n_rep).reshape(n_rep * rows, feat_dev)
    gathered_grad = hier_gather(grad_agg)
    feature_grad = block_product(adjacency_tiles, positions, gathered_grad)
    weight_part = jnp.einsum("irf,ro->ifo", agg_rows, grad_pre, preferred_element_type=jnp.float32)
    weight_rows = halving_scatter(weight_part, REP, n_rep)
    node_total = node_features.shape[0] * n_blk
    weight_grad = butterfly_sum(weight_rows, BLK, n_blk) * (1.0 / math.sqrt(node_total))
    return (activated, feature_grad, weight_grad)


def solution(mesh):
    n_blk, n_rep = mesh.shape["blk"], mesh.shape["rep"]
    sizes = (n_blk // 8, 2, 4, n_rep // 2, 2)
    fine = Mesh(mesh.devices.reshape(sizes), BLK + REP)
    return jax.shard_map(
        functools.partial(local, sizes),
        mesh=fine,
        in_specs=(
            P(BLK, REP),
            P(),
            P(BLK + REP, None),
            P(BLK, None, None, None),
            P(BLK, None),
            P(),
        ),
        out_specs=(P(BLK + REP, None), P(BLK, REP), P(REP, None)),
        check_vma=False,
    )
```

```python
import functools
import math

import jax
import jax.numpy as jnp
from jax import lax
from jax.experimental import pallas as pl
from jax.experimental.pallas import tpu as pltpu
from jax.sharding import Mesh, PartitionSpec as P


def column_positions(block_cols, block_perm):
    numbers = jnp.arange(block_perm.shape[0], dtype=jnp.int32)
    matches = block_cols[:, :, None] == numbers[None, None, :]
    return jnp.sum(jnp.where(matches, block_perm[None, None, :], 0), axis=-1)


def _product_kernel(pos_ref, a_ref, x_ref, o_ref):
    p = pl.program_id(0)
    tiles = a_ref.shape[1]
    lhs = jnp.concatenate([a_ref[0, k] for k in range(tiles)], axis=1)
    rhs = jnp.concatenate([x_ref[pos_ref[p * tiles + k]] for k in range(tiles)], axis=0)
    o_ref[0] = jnp.dot(lhs, rhs, preferred_element_type=jnp.float32).astype(o_ref.dtype)


def block_product(adjacency_tiles, positions, gathered):
    rows, tiles, bs, _ = adjacency_tiles.shape
    width = gathered.shape[1]
    blocks = gathered.reshape(-1, bs, width)
    cost = pl.CostEstimate(
        flops=2 * rows * tiles * bs * bs * width,
        bytes_accessed=2 * rows * tiles * bs * bs + 2 * blocks.size + 2 * rows * bs * width,
        transcendentals=0,
    )
    out = pl.pallas_call(
        _product_kernel,
        grid_spec=pltpu.PrefetchScalarGridSpec(
            num_scalar_prefetch=1,
            grid=(rows,),
            in_specs=[
                pl.BlockSpec((1, tiles, bs, bs), lambda p, pos: (p, 0, 0, 0)),
                pl.BlockSpec(blocks.shape, lambda p, pos: (0, 0, 0), pipeline_mode=pl.Buffered(1)),
            ],
            out_specs=pl.BlockSpec((1, bs, width), lambda p, pos: (p, 0, 0)),
        ),
        out_shape=jax.ShapeDtypeStruct((rows, bs, width), jnp.bfloat16),
        compiler_params=pltpu.CompilerParams(
            dimension_semantics=("arbitrary",), vmem_limit_bytes=48 * 1024 * 1024
        ),
        cost_estimate=cost,
    )(positions.reshape(-1), adjacency_tiles, blocks)
    return out.reshape(rows * bs, width)


def xor_pairs(size, bit):
    return [(i, i ^ bit) for i in range(size)]


def butterfly_sum(x, axis, size):
    bit = 1
    while bit < size:
        x = x + lax.ppermute(x, axis, xor_pairs(size, bit))
        bit *= 2
    return x


def halving_scatter(parts, axis, size):
    me = lax.axis_index(axis)
    bit = size // 2
    while bit >= 1:
        half = parts.shape[0] // 2
        lo, hi = parts[:half], parts[half:]
        mine_hi = (me & bit) != 0
        keep = jnp.where(mine_hi, hi, lo)
        send = jnp.where(mine_hi, lo, hi)
        parts = keep + lax.ppermute(send, axis, xor_pairs(size, bit))
        bit //= 2
    return parts[0]


BLK = ("z", "xh", "y")
REP = ("xl", "c")


def exchange(parts, size, far=False):
    me = lax.axis_index(REP)
    axis = ("xh",) + REP if far else REP
    got = []
    for s in range(size):
        send = lax.dynamic_index_in_dim(parts, me ^ s, 0, keepdims=False)
        if far:
            send = lax.ppermute(send, axis, xor_pairs(2 * size, size + s))
        elif s:
            send = lax.ppermute(send, axis, xor_pairs(size, s))
        got.append(send)
    return jnp.take(jnp.stack(got), jnp.arange(size) ^ me, axis=0)


def hier_gather(x):
    partner = lax.ppermute(x, "xh", xor_pairs(2, 1))
    pair = jnp.concatenate([x, partner], axis=0)
    return lax.all_gather(pair, ("z", "y"), axis=0, tiled=True)


def hier_positions(positions, local_blocks, n_xh, n_y):
    owner, block = positions // local_blocks, positions % local_blocks
    z, xh, y = owner // (n_xh * n_y), (owner // n_y) % n_xh, owner % n_y
    slot = xh ^ lax.axis_index("xh")
    return ((z * n_y + y) * n_xh + slot) * local_blocks + block


def local(sizes, node_features, weight, cotangent, adjacency_tiles, block_cols, block_perm):
    n_z, n_xh, n_y, n_xl, n_c = sizes
    n_blk, n_rep = n_z * n_xh * n_y, n_xl * n_c
    feat_dev = node_features.shape[1]
    f_all = weight.shape[0]
    bs = adjacency_tiles.shape[2]
    w_split = weight.reshape(n_rep, feat_dev, f_all)
    positions = column_positions(block_cols, block_perm)
    positions = hier_positions(positions, node_features.shape[0] // bs, n_xh, n_y)
    gathered = hier_gather(node_features)
    aggregate = block_product(adjacency_tiles, positions, gathered)
    rows = aggregate.shape[0] // n_rep
    agg_rows = exchange(aggregate.reshape(n_rep, rows, feat_dev), n_rep)
    preact = jnp.einsum("irf,ifo->ro", agg_rows, w_split, preferred_element_type=jnp.float32)
    gating = jax.nn.sigmoid(preact)
    activated = (preact * gating).astype(jnp.bfloat16)
    slopes = gating * (1.0 + preact * (1.0 - gating))
    grad_pre = (cotangent.astype(jnp.float32) * slopes).astype(jnp.bfloat16)
    grad_split = jnp.einsum(
        "rf,jof->jro", grad_pre, w_split, preferred_element_type=jnp.float32
    ).astype(jnp.bfloat16)
    pair = jnp.concatenate([exchange(grad_split, n_rep), exchange(grad_split, n_rep, far=True)])
    gathered_grad = lax.all_gather(pair.reshape(-1, feat_dev), ("z", "y"), axis=0, tiled=True)
    feature_grad = block_product(adjacency_tiles, positions, gathered_grad)
    weight_part = jnp.einsum("irf,ro->ifo", agg_rows, grad_pre, preferred_element_type=jnp.float32)
    weight_rows = halving_scatter(weight_part, REP, n_rep)
    node_total = node_features.shape[0] * n_blk
    weight_grad = butterfly_sum(weight_rows, BLK, n_blk) * (1.0 / math.sqrt(node_total))
    return (activated, feature_grad, weight_grad)


def solution(mesh):
    n_blk, n_rep = mesh.shape["blk"], mesh.shape["rep"]
    sizes = (n_blk // 8, 2, 4, n_rep // 2, 2)
    fine = Mesh(mesh.devices.reshape(sizes), BLK + REP)
    return jax.shard_map(
        functools.partial(local, sizes),
        mesh=fine,
        in_specs=(
            P(BLK, REP),
            P(),
            P(BLK + REP, None),
            P(BLK, None, None, None),
            P(BLK, None),
            P(),
        ),
        out_specs=(P(BLK + REP, None), P(BLK, REP), P(REP, None)),
        check_vma=False,
    )
```

```python
import functools
import math

import jax
import jax.numpy as jnp
from jax import lax
from jax.experimental import pallas as pl
from jax.experimental.pallas import tpu as pltpu
from jax.sharding import Mesh, PartitionSpec as P


def column_positions(block_cols, block_perm):
    numbers = jnp.arange(block_perm.shape[0], dtype=jnp.int32)
    matches = block_cols[:, :, None] == numbers[None, None, :]
    return jnp.sum(jnp.where(matches, block_perm[None, None, :], 0), axis=-1)


def _product_kernel(pos_ref, a_ref, x_ref, o_ref):
    step = pl.program_id(0)
    group, tiles = a_ref.shape[0], a_ref.shape[1]
    for g in range(group):
        base = (step * group + g) * tiles
        lhs = jnp.concatenate([a_ref[g, k] for k in range(tiles)], axis=1)
        rhs = jnp.concatenate([x_ref[pos_ref[base + k]] for k in range(tiles)], axis=0)
        o_ref[g] = jnp.dot(lhs, rhs, preferred_element_type=jnp.float32).astype(o_ref.dtype)


def block_product(adjacency_tiles, positions, gathered):
    rows, tiles, bs, _ = adjacency_tiles.shape
    width = gathered.shape[1]
    group = 2 if rows % 2 == 0 else 1
    blocks = gathered.reshape(-1, bs, width)
    cost = pl.CostEstimate(
        flops=2 * rows * tiles * bs * bs * width,
        bytes_accessed=2 * rows * tiles * bs * bs + 2 * blocks.size + 2 * rows * bs * width,
        transcendentals=0,
    )
    out = pl.pallas_call(
        _product_kernel,
        grid_spec=pltpu.PrefetchScalarGridSpec(
            num_scalar_prefetch=1,
            grid=(rows // group,),
            in_specs=[
                pl.BlockSpec((group, tiles, bs, bs), lambda p, pos: (p, 0, 0, 0)),
                pl.BlockSpec(blocks.shape, lambda p, pos: (0, 0, 0), pipeline_mode=pl.Buffered(1)),
            ],
            out_specs=pl.BlockSpec((group, bs, width), lambda p, pos: (p, 0, 0)),
        ),
        out_shape=jax.ShapeDtypeStruct((rows, bs, width), jnp.bfloat16),
        compiler_params=pltpu.CompilerParams(
            dimension_semantics=("arbitrary",), vmem_limit_bytes=48 * 1024 * 1024
        ),
        cost_estimate=cost,
    )(positions.reshape(-1), adjacency_tiles, blocks)
    return out.reshape(rows * bs, width)


def xor_pairs(size, bit):
    return [(i, i ^ bit) for i in range(size)]


def butterfly_sum(x, axis, size):
    bit = 1
    while bit < size:
        x = x + lax.ppermute(x, axis, xor_pairs(size, bit))
        bit *= 2
    return x


def halving_scatter(parts, axis, size):
    me = lax.axis_index(axis)
    bit = size // 2
    while bit >= 1:
        half = parts.shape[0] // 2
        lo, hi = parts[:half], parts[half:]
        mine_hi = (me & bit) != 0
        keep = jnp.where(mine_hi, hi, lo)
        send = jnp.where(mine_hi, lo, hi)
        parts = keep + lax.ppermute(send, axis, xor_pairs(size, bit))
        bit //= 2
    return parts[0]


BLK = ("z", "xh", "y")
REP = ("xl", "c")


def exchange(parts, size, far=False):
    me = lax.axis_index(REP)
    axis = ("xh",) + REP if far else REP
    got = []
    for s in range(size):
        send = lax.dynamic_index_in_dim(parts, me ^ s, 0, keepdims=False)
        if far:
            send = lax.ppermute(send, axis, xor_pairs(2 * size, size + s))
        elif s:
            send = lax.ppermute(send, axis, xor_pairs(size, s))
        got.append(send)
    return jnp.take(jnp.stack(got), jnp.arange(size) ^ me, axis=0)


def hier_gather(x):
    pieces = jnp.split(x, 4, axis=0)
    partner = [lax.ppermute(piece, "xh", xor_pairs(2, 1)) for piece in pieces]
    pair = jnp.concatenate([x] + partner, axis=0)
    return lax.all_gather(pair, ("z", "y"), axis=0, tiled=True)


def hier_positions(positions, local_blocks, n_xh, n_y):
    owner, block = positions // local_blocks, positions % local_blocks
    z, xh, y = owner // (n_xh * n_y), (owner // n_y) % n_xh, owner % n_y
    slot = xh ^ lax.axis_index("xh")
    return ((z * n_y + y) * n_xh + slot) * local_blocks + block


def local(sizes, node_features, weight, cotangent, adjacency_tiles, block_cols, block_perm):
    n_z, n_xh, n_y, n_xl, n_c = sizes
    n_blk, n_rep = n_z * n_xh * n_y, n_xl * n_c
    feat_dev = node_features.shape[1]
    f_all = weight.shape[0]
    bs = adjacency_tiles.shape[2]
    w_split = weight.reshape(n_rep, feat_dev, f_all)
    positions = column_positions(block_cols, block_perm)
    positions = hier_positions(positions, node_features.shape[0] // bs, n_xh, n_y)
    gathered = hier_gather(node_features)
    aggregate = block_product(adjacency_tiles, positions, gathered)
    rows = aggregate.shape[0] // n_rep
    agg_rows = exchange(aggregate.reshape(n_rep, rows, feat_dev), n_rep)
    preact = jnp.einsum("irf,ifo->ro", agg_rows, w_split, preferred_element_type=jnp.float32)
    gating = jax.nn.sigmoid(preact)
    activated = (preact * gating).astype(jnp.bfloat16)
    slopes = gating * (1.0 + preact * (1.0 - gating))
    grad_pre = (cotangent.astype(jnp.float32) * slopes).astype(jnp.bfloat16)
    grad_split = jnp.einsum(
        "rf,jof->jro", grad_pre, w_split, preferred_element_type=jnp.float32
    ).astype(jnp.bfloat16)
    pair = jnp.concatenate([exchange(grad_split, n_rep), exchange(grad_split, n_rep, far=True)])
    gathered_grad = lax.all_gather(pair.reshape(-1, feat_dev), ("z", "y"), axis=0, tiled=True)
    feature_grad = block_product(adjacency_tiles, positions, gathered_grad)
    weight_part = jnp.einsum("irf,ro->ifo", agg_rows, grad_pre, preferred_element_type=jnp.float32)
    weight_rows = halving_scatter(weight_part, REP, n_rep)
    node_total = node_features.shape[0] * n_blk
    weight_grad = butterfly_sum(weight_rows, BLK, n_blk) * (1.0 / math.sqrt(node_total))
    return (activated, feature_grad, weight_grad)


def solution(mesh):
    n_blk, n_rep = mesh.shape["blk"], mesh.shape["rep"]
    sizes = (n_blk // 8, 2, 4, n_rep // 2, 2)
    fine = Mesh(mesh.devices.reshape(sizes), BLK + REP)
    return jax.shard_map(
        functools.partial(local, sizes),
        mesh=fine,
        in_specs=(
            P(BLK, REP),
            P(),
            P(BLK + REP, None),
            P(BLK, None, None, None),
            P(BLK, None),
            P(),
        ),
        out_specs=(P(BLK + REP, None), P(BLK, REP), P(REP, None)),
        check_vma=False,
    )
```

```python
import functools
import math

import jax
import jax.numpy as jnp
from jax import lax
from jax.experimental import pallas as pl
from jax.experimental.pallas import tpu as pltpu
from jax.sharding import Mesh, PartitionSpec as P


def column_positions(block_cols, block_perm):
    numbers = jnp.arange(block_perm.shape[0], dtype=jnp.int32)
    matches = block_cols[:, :, None] == numbers[None, None, :]
    return jnp.sum(jnp.where(matches, block_perm[None, None, :], 0), axis=-1)


def _product_kernel(pos_ref, a_ref, x_ref, o_ref):
    step = pl.program_id(0)
    group, tiles = a_ref.shape[0], a_ref.shape[1]
    for g in range(group):
        base = (step * group + g) * tiles
        lhs = jnp.concatenate([a_ref[g, k] for k in range(tiles)], axis=1)
        rhs = jnp.concatenate([x_ref[pos_ref[base + k]] for k in range(tiles)], axis=0)
        o_ref[g] = jnp.dot(lhs, rhs, preferred_element_type=jnp.float32).astype(o_ref.dtype)


def block_product(adjacency_tiles, positions, gathered):
    rows, tiles, bs, _ = adjacency_tiles.shape
    width = gathered.shape[1]
    group = 4 if rows % 4 == 0 else 1
    blocks = gathered.reshape(-1, bs, width)
    cost = pl.CostEstimate(
        flops=2 * rows * tiles * bs * bs * width,
        bytes_accessed=2 * rows * tiles * bs * bs + 2 * blocks.size + 2 * rows * bs * width,
        transcendentals=0,
    )
    out = pl.pallas_call(
        _product_kernel,
        grid_spec=pltpu.PrefetchScalarGridSpec(
            num_scalar_prefetch=1,
            grid=(rows // group,),
            in_specs=[
                pl.BlockSpec((group, tiles, bs, bs), lambda p, pos: (p, 0, 0, 0)),
                pl.BlockSpec(blocks.shape, lambda p, pos: (0, 0, 0), pipeline_mode=pl.Buffered(1)),
            ],
            out_specs=pl.BlockSpec((group, bs, width), lambda p, pos: (p, 0, 0)),
        ),
        out_shape=jax.ShapeDtypeStruct((rows, bs, width), jnp.bfloat16),
        compiler_params=pltpu.CompilerParams(
            dimension_semantics=("arbitrary",), vmem_limit_bytes=48 * 1024 * 1024
        ),
        cost_estimate=cost,
    )(positions.reshape(-1), adjacency_tiles, blocks)
    return out.reshape(rows * bs, width)


def xor_pairs(size, bit):
    return [(i, i ^ bit) for i in range(size)]


def butterfly_sum(x, axis, size):
    bit = 1
    while bit < size:
        x = x + lax.ppermute(x, axis, xor_pairs(size, bit))
        bit *= 2
    return x


def halving_scatter(parts, axis, size):
    me = lax.axis_index(axis)
    bit = size // 2
    while bit >= 1:
        half = parts.shape[0] // 2
        lo, hi = parts[:half], parts[half:]
        mine_hi = (me & bit) != 0
        keep = jnp.where(mine_hi, hi, lo)
        send = jnp.where(mine_hi, lo, hi)
        parts = keep + lax.ppermute(send, axis, xor_pairs(size, bit))
        bit //= 2
    return parts[0]


BLK = ("z", "xh", "y")
REP = ("xl", "c")


def exchange(parts, size, far=False):
    me = lax.axis_index(REP)
    axis = ("xh",) + REP if far else REP
    got = []
    for s in range(size):
        send = lax.dynamic_index_in_dim(parts, me ^ s, 0, keepdims=False)
        if far:
            send = lax.ppermute(send, axis, xor_pairs(2 * size, size + s))
        elif s:
            send = lax.ppermute(send, axis, xor_pairs(size, s))
        got.append(send)
    return jnp.take(jnp.stack(got), jnp.arange(size) ^ me, axis=0)


def hier_gather(x):
    pieces = jnp.split(x, 4, axis=0)
    partner = [lax.ppermute(piece, "xh", xor_pairs(2, 1)) for piece in pieces]
    pair = jnp.concatenate([x] + partner, axis=0)
    return lax.all_gather(pair, ("y", "z"), axis=0, tiled=True)


def hier_positions(positions, local_blocks, n_z, n_xh, n_y):
    owner, block = positions // local_blocks, positions % local_blocks
    z, xh, y = owner // (n_xh * n_y), (owner // n_y) % n_xh, owner % n_y
    slot = xh ^ lax.axis_index("xh")
    return ((y * n_z + z) * n_xh + slot) * local_blocks + block


def local(sizes, node_features, weight, cotangent, adjacency_tiles, block_cols, block_perm):
    n_z, n_xh, n_y, n_xl, n_c = sizes
    n_blk, n_rep = n_z * n_xh * n_y, n_xl * n_c
    feat_dev = node_features.shape[1]
    f_all = weight.shape[0]
    bs = adjacency_tiles.shape[2]
    w_split = weight.reshape(n_rep, feat_dev, f_all)
    positions = column_positions(block_cols, block_perm)
    positions = hier_positions(positions, node_features.shape[0] // bs, n_z, n_xh, n_y)
    gathered = hier_gather(node_features)
    aggregate = block_product(adjacency_tiles, positions, gathered)
    rows = aggregate.shape[0] // n_rep
    agg_rows = exchange(aggregate.reshape(n_rep, rows, feat_dev), n_rep)
    preact = jnp.einsum("irf,ifo->ro", agg_rows, w_split, preferred_element_type=jnp.float32)
    gating = jax.nn.sigmoid(preact)
    activated = (preact * gating).astype(jnp.bfloat16)
    slopes = gating * (1.0 + preact * (1.0 - gating))
    grad_pre = (cotangent.astype(jnp.float32) * slopes).astype(jnp.bfloat16)
    grad_split = jnp.einsum(
        "rf,jof->jro", grad_pre, w_split, preferred_element_type=jnp.float32
    ).astype(jnp.bfloat16)
    pair = jnp.concatenate([exchange(grad_split, n_rep), exchange(grad_split, n_rep, far=True)])
    gathered_grad = lax.all_gather(pair.reshape(-1, feat_dev), ("y", "z"), axis=0, tiled=True)
    feature_grad = block_product(adjacency_tiles, positions, gathered_grad)
    weight_part = jnp.einsum("irf,ro->ifo", agg_rows, grad_pre, preferred_element_type=jnp.float32)
    weight_rows = halving_scatter(weight_part, REP, n_rep)
    node_total = node_features.shape[0] * n_blk
    weight_grad = butterfly_sum(weight_rows, BLK, n_blk) * (1.0 / math.sqrt(node_total))
    return (activated, feature_grad, weight_grad)


def solution(mesh):
    n_blk, n_rep = mesh.shape["blk"], mesh.shape["rep"]
    sizes = (n_blk // 8, 2, 4, n_rep // 2, 2)
    fine = Mesh(mesh.devices.reshape(sizes), BLK + REP)
    return jax.shard_map(
        functools.partial(local, sizes),
        mesh=fine,
        in_specs=(
            P(BLK, REP),
            P(),
            P(BLK + REP, None),
            P(BLK, None, None, None),
            P(BLK, None),
            P(),
        ),
        out_specs=(P(BLK + REP, None), P(BLK, REP), P(REP, None)),
        check_vma=False,
    )
```

```python
import functools
import math

import jax
import jax.numpy as jnp
from jax import lax
from jax.experimental import pallas as pl
from jax.experimental.pallas import tpu as pltpu
from jax.sharding import Mesh, PartitionSpec as P


def column_positions(block_cols, block_perm):
    numbers = jnp.arange(block_perm.shape[0], dtype=jnp.int32)
    matches = block_cols[:, :, None] == numbers[None, None, :]
    return jnp.sum(jnp.where(matches, block_perm[None, None, :], 0), axis=-1)


def _product_kernel(pos_ref, a_ref, x_ref, o_ref):
    step = pl.program_id(0)
    group, tiles = a_ref.shape[0], a_ref.shape[1]
    for g in range(group):
        base = (step * group + g) * tiles
        lhs = jnp.concatenate([a_ref[g, k] for k in range(tiles)], axis=1)
        rhs = jnp.concatenate([x_ref[pos_ref[base + k]] for k in range(tiles)], axis=0)
        o_ref[g] = jnp.dot(lhs, rhs, preferred_element_type=jnp.float32).astype(o_ref.dtype)


def block_product(adjacency_tiles, positions, gathered):
    rows, tiles, bs, _ = adjacency_tiles.shape
    width = gathered.shape[1]
    group = 4 if rows % 4 == 0 else 1
    blocks = gathered.reshape(-1, bs, width)
    cost = pl.CostEstimate(
        flops=2 * rows * tiles * bs * bs * width,
        bytes_accessed=2 * rows * tiles * bs * bs + 2 * blocks.size + 2 * rows * bs * width,
        transcendentals=0,
    )
    out = pl.pallas_call(
        _product_kernel,
        grid_spec=pltpu.PrefetchScalarGridSpec(
            num_scalar_prefetch=1,
            grid=(rows // group,),
            in_specs=[
                pl.BlockSpec((group, tiles, bs, bs), lambda p, pos: (p, 0, 0, 0)),
                pl.BlockSpec(blocks.shape, lambda p, pos: (0, 0, 0), pipeline_mode=pl.Buffered(1)),
            ],
            out_specs=pl.BlockSpec((group, bs, width), lambda p, pos: (p, 0, 0)),
        ),
        out_shape=jax.ShapeDtypeStruct((rows, bs, width), jnp.bfloat16),
        compiler_params=pltpu.CompilerParams(
            dimension_semantics=("arbitrary",), vmem_limit_bytes=48 * 1024 * 1024
        ),
        cost_estimate=cost,
    )(positions.reshape(-1), adjacency_tiles, blocks)
    return out.reshape(rows * bs, width)


def xor_pairs(size, bit):
    return [(i, i ^ bit) for i in range(size)]


def butterfly_sum(x, axis, size):
    bit = 1
    while bit < size:
        x = x + lax.ppermute(x, axis, xor_pairs(size, bit))
        bit *= 2
    return x


def halving_scatter(parts, axis, size):
    me = lax.axis_index(axis)
    bit = size // 2
    while bit >= 1:
        half = parts.shape[0] // 2
        lo, hi = parts[:half], parts[half:]
        mine_hi = (me & bit) != 0
        keep = jnp.where(mine_hi, hi, lo)
        send = jnp.where(mine_hi, lo, hi)
        parts = keep + lax.ppermute(send, axis, xor_pairs(size, bit))
        bit //= 2
    return parts[0]


BLK = ("z", "xh", "y")
REP = ("xl", "c")


def exchange(parts, size, far=False):
    me = lax.axis_index(REP)
    axis = ("xh",) + REP if far else REP
    got = []
    for s in range(size):
        send = lax.dynamic_index_in_dim(parts, me ^ s, 0, keepdims=False)
        if far:
            send = lax.ppermute(send, axis, xor_pairs(2 * size, size + s))
        elif s:
            send = lax.ppermute(send, axis, xor_pairs(size, s))
        got.append(send)
    return jnp.take(jnp.stack(got), jnp.arange(size) ^ me, axis=0)


def hier_gather(x):
    pieces = jnp.split(x, 4, axis=0)
    partner = [lax.ppermute(piece, "xh", xor_pairs(2, 1)) for piece in pieces]
    pair = jnp.concatenate([x] + partner, axis=0)
    return lax.all_gather(pair, ("y", "z"), axis=0, tiled=True)


def hier_positions(positions, local_blocks, n_z, n_xh, n_y):
    owner, block = positions // local_blocks, positions % local_blocks
    z, xh, y = owner // (n_xh * n_y), (owner // n_y) % n_xh, owner % n_y
    slot = xh ^ lax.axis_index("xh")
    return ((y * n_z + z) * n_xh + slot) * local_blocks + block


def flat_positions(positions, local_blocks, n_z, n_xh, n_y):
    owner, block = positions // local_blocks, positions % local_blocks
    z, xh, y = owner // (n_xh * n_y), (owner // n_y) % n_xh, owner % n_y
    return ((xh * n_y + y) * n_z + z) * local_blocks + block


def local(sizes, node_features, weight, cotangent, adjacency_tiles, block_cols, block_perm):
    n_z, n_xh, n_y, n_xl, n_c = sizes
    n_blk, n_rep = n_z * n_xh * n_y, n_xl * n_c
    feat_dev = node_features.shape[1]
    f_all = weight.shape[0]
    bs = adjacency_tiles.shape[2]
    w_split = weight.reshape(n_rep, feat_dev, f_all)
    positions = column_positions(block_cols, block_perm)
    raw, lb = positions, node_features.shape[0] // bs
    positions = hier_positions(raw, lb, n_z, n_xh, n_y)
    gathered = lax.all_gather(node_features, ("xh", "y", "z"), axis=0, tiled=True)
    aggregate = block_product(adjacency_tiles, flat_positions(raw, lb, n_z, n_xh, n_y), gathered)
    rows = aggregate.shape[0] // n_rep
    agg_rows = exchange(aggregate.reshape(n_rep, rows, feat_dev), n_rep)
    preact = jnp.einsum("irf,ifo->ro", agg_rows, w_split, preferred_element_type=jnp.float32)
    gating = jax.nn.sigmoid(preact)
    activated = (preact * gating).astype(jnp.bfloat16)
    slopes = gating * (1.0 + preact * (1.0 - gating))
    grad_pre = (cotangent.astype(jnp.float32) * slopes).astype(jnp.bfloat16)
    grad_split = jnp.einsum(
        "rf,jof->jro", grad_pre, w_split, preferred_element_type=jnp.float32
    ).astype(jnp.bfloat16)
    pair = jnp.concatenate([exchange(grad_split, n_rep), exchange(grad_split, n_rep, far=True)])
    gathered_grad = lax.all_gather(pair.reshape(-1, feat_dev), ("y", "z"), axis=0, tiled=True)
    feature_grad = block_product(adjacency_tiles, positions, gathered_grad)
    weight_part = jnp.einsum("irf,ro->ifo", agg_rows, grad_pre, preferred_element_type=jnp.float32)
    weight_rows = halving_scatter(weight_part, REP, n_rep)
    node_total = node_features.shape[0] * n_blk
    weight_grad = butterfly_sum(weight_rows, BLK, n_blk) * (1.0 / math.sqrt(node_total))
    return (activated, feature_grad, weight_grad)


def solution(mesh):
    n_blk, n_rep = mesh.shape["blk"], mesh.shape["rep"]
    sizes = (n_blk // 8, 2, 4, n_rep // 2, 2)
    fine = Mesh(mesh.devices.reshape(sizes), BLK + REP)
    return jax.shard_map(
        functools.partial(local, sizes),
        mesh=fine,
        in_specs=(
            P(BLK, REP),
            P(),
            P(BLK + REP, None),
            P(BLK, None, None, None),
            P(BLK, None),
            P(),
        ),
        out_specs=(P(BLK + REP, None), P(BLK, REP), P(REP, None)),
        check_vma=False,
    )
```

```python
import functools
import math

import jax
import jax.numpy as jnp
from jax import lax
from jax.experimental import pallas as pl
from jax.experimental.pallas import tpu as pltpu
from jax.sharding import Mesh, PartitionSpec as P


def column_positions(block_cols, block_perm):
    numbers = jnp.arange(block_perm.shape[0], dtype=jnp.int32)
    matches = block_cols[:, :, None] == numbers[None, None, :]
    return jnp.sum(jnp.where(matches, block_perm[None, None, :], 0), axis=-1)


def _product_kernel(pos_ref, a_ref, x_ref, o_ref):
    step = pl.program_id(0)
    group, tiles = a_ref.shape[0], a_ref.shape[1]
    for g in range(group):
        base = (step * group + g) * tiles
        lhs = jnp.concatenate([a_ref[g, k] for k in range(tiles)], axis=1)
        rhs = jnp.concatenate([x_ref[pos_ref[base + k]] for k in range(tiles)], axis=0)
        o_ref[g] = jnp.dot(lhs, rhs, preferred_element_type=jnp.float32).astype(o_ref.dtype)


def block_product(adjacency_tiles, positions, gathered):
    rows, tiles, bs, _ = adjacency_tiles.shape
    width = gathered.shape[1]
    group = 4 if rows % 4 == 0 else 1
    blocks = gathered.reshape(-1, bs, width)
    cost = pl.CostEstimate(
        flops=2 * rows * tiles * bs * bs * width,
        bytes_accessed=2 * rows * tiles * bs * bs + 2 * blocks.size + 2 * rows * bs * width,
        transcendentals=0,
    )
    out = pl.pallas_call(
        _product_kernel,
        grid_spec=pltpu.PrefetchScalarGridSpec(
            num_scalar_prefetch=1,
            grid=(rows // group,),
            in_specs=[
                pl.BlockSpec((group, tiles, bs, bs), lambda p, pos: (p, 0, 0, 0)),
                pl.BlockSpec(blocks.shape, lambda p, pos: (0, 0, 0), pipeline_mode=pl.Buffered(1)),
            ],
            out_specs=pl.BlockSpec((group, bs, width), lambda p, pos: (p, 0, 0)),
        ),
        out_shape=jax.ShapeDtypeStruct((rows, bs, width), jnp.bfloat16),
        compiler_params=pltpu.CompilerParams(
            dimension_semantics=("arbitrary",), vmem_limit_bytes=48 * 1024 * 1024
        ),
        cost_estimate=cost,
    )(positions.reshape(-1), adjacency_tiles, blocks)
    return out.reshape(rows * bs, width)


def xor_pairs(size, bit):
    return [(i, i ^ bit) for i in range(size)]


def butterfly_sum(x, axis, size):
    bit = 1
    while bit < size:
        x = x + lax.ppermute(x, axis, xor_pairs(size, bit))
        bit *= 2
    return x


def halving_scatter(parts, axis, size):
    me = lax.axis_index(axis)
    bit = size // 2
    while bit >= 1:
        half = parts.shape[0] // 2
        lo, hi = parts[:half], parts[half:]
        mine_hi = (me & bit) != 0
        keep = jnp.where(mine_hi, hi, lo)
        send = jnp.where(mine_hi, lo, hi)
        parts = keep + lax.ppermute(send, axis, xor_pairs(size, bit))
        bit //= 2
    return parts[0]


BLK = ("z", "xh", "y")
REP = ("xl", "c")


def exchange(parts, size, far=False, ordered=True):
    me = lax.axis_index(REP)
    axis = ("xh",) + REP if far else REP
    got = []
    for s in range(size):
        send = lax.dynamic_index_in_dim(parts, me ^ s, 0, keepdims=False)
        if far:
            send = lax.ppermute(send, axis, xor_pairs(2 * size, size + s))
        elif s:
            send = lax.ppermute(send, axis, xor_pairs(size, s))
        got.append(send)
    got = jnp.stack(got)
    return jnp.take(got, jnp.arange(size) ^ me, axis=0) if ordered else got


def hier_gather(x):
    pieces = jnp.split(x, 4, axis=0)
    partner = [lax.ppermute(piece, "xh", xor_pairs(2, 1)) for piece in pieces]
    pair = jnp.concatenate([x] + partner, axis=0)
    return lax.all_gather(pair, ("y", "z"), axis=0, tiled=True)


def hier_positions(positions, local_blocks, n_z, n_xh, n_y, piece_blocks=None):
    owner, block = positions // local_blocks, positions % local_blocks
    if piece_blocks:
        piece = (block // piece_blocks) ^ lax.axis_index(REP)
        block = piece * piece_blocks + block % piece_blocks
    z, xh, y = owner // (n_xh * n_y), (owner // n_y) % n_xh, owner % n_y
    slot = xh ^ lax.axis_index("xh")
    return ((y * n_z + z) * n_xh + slot) * local_blocks + block


def local(sizes, node_features, weight, cotangent, adjacency_tiles, block_cols, block_perm):
    n_z, n_xh, n_y, n_xl, n_c = sizes
    n_blk, n_rep = n_z * n_xh * n_y, n_xl * n_c
    feat_dev = node_features.shape[1]
    f_all = weight.shape[0]
    bs = adjacency_tiles.shape[2]
    w_split = weight.reshape(n_rep, feat_dev, f_all)
    positions = column_positions(block_cols, block_perm)
    raw, lb = positions, node_features.shape[0] // bs
    positions = hier_positions(raw, lb, n_z, n_xh, n_y)
    gathered = hier_gather(node_features)
    aggregate = block_product(adjacency_tiles, positions, gathered)
    rows = aggregate.shape[0] // n_rep
    flip = jnp.arange(n_rep) ^ lax.axis_index(REP)
    agg_got = exchange(aggregate.reshape(n_rep, rows, feat_dev), n_rep, ordered=False)
    w_got = jnp.take(w_split, flip, axis=0)
    preact = jnp.einsum("irf,ifo->ro", agg_got, w_got, preferred_element_type=jnp.float32)
    gating = jax.nn.sigmoid(preact)
    activated = (preact * gating).astype(jnp.bfloat16)
    slopes = gating * (1.0 + preact * (1.0 - gating))
    grad_pre = (cotangent.astype(jnp.float32) * slopes).astype(jnp.bfloat16)
    grad_split = jnp.einsum(
        "rf,jof->jro", grad_pre, w_split, preferred_element_type=jnp.float32
    ).astype(jnp.bfloat16)
    own = exchange(grad_split, n_rep, ordered=False)
    far = exchange(grad_split, n_rep, far=True, ordered=False)
    pair = jnp.concatenate([own, far])
    gathered_grad = lax.all_gather(pair.reshape(-1, feat_dev), ("y", "z"), axis=0, tiled=True)
    grad_positions = hier_positions(raw, lb, n_z, n_xh, n_y, rows // bs)
    feature_grad = block_product(adjacency_tiles, grad_positions, gathered_grad)
    agg_rows = jnp.take(agg_got, flip, axis=0)
    weight_part = jnp.einsum("irf,ro->ifo", agg_rows, grad_pre, preferred_element_type=jnp.float32)
    weight_rows = halving_scatter(weight_part, REP, n_rep)
    node_total = node_features.shape[0] * n_blk
    weight_grad = butterfly_sum(weight_rows, BLK, n_blk) * (1.0 / math.sqrt(node_total))
    return (activated, feature_grad, weight_grad)


def solution(mesh):
    n_blk, n_rep = mesh.shape["blk"], mesh.shape["rep"]
    sizes = (n_blk // 8, 2, 4, n_rep // 2, 2)
    fine = Mesh(mesh.devices.reshape(sizes), BLK + REP)
    return jax.shard_map(
        functools.partial(local, sizes),
        mesh=fine,
        in_specs=(
            P(BLK, REP),
            P(),
            P(BLK + REP, None),
            P(BLK, None, None, None),
            P(BLK, None),
            P(),
        ),
        out_specs=(P(BLK + REP, None), P(BLK, REP), P(REP, None)),
        check_vma=False,
    )
```

```python
import functools
import math

import jax
import jax.numpy as jnp
from jax import lax
from jax.experimental import pallas as pl
from jax.experimental.pallas import tpu as pltpu
from jax.sharding import Mesh, PartitionSpec as P


def column_positions(block_cols, block_perm):
    numbers = jnp.arange(block_perm.shape[0], dtype=jnp.int32)
    matches = block_cols[:, :, None] == numbers[None, None, :]
    return jnp.sum(jnp.where(matches, block_perm[None, None, :], 0), axis=-1)


def _product_kernel(pos_ref, a_ref, x_ref, o_ref):
    step = pl.program_id(0)
    group, tiles = a_ref.shape[0], a_ref.shape[1]
    for g in range(group):
        base = (step * group + g) * tiles
        lhs = jnp.concatenate([a_ref[g, k] for k in range(tiles)], axis=1)
        rhs = jnp.concatenate([x_ref[pos_ref[base + k]] for k in range(tiles)], axis=0)
        o_ref[g] = jnp.dot(lhs, rhs, preferred_element_type=jnp.float32).astype(o_ref.dtype)


def block_product(adjacency_tiles, positions, gathered):
    rows, tiles, bs, _ = adjacency_tiles.shape
    width = gathered.shape[1]
    group = 4 if rows % 4 == 0 else 1
    blocks = gathered.reshape(-1, bs, width)
    cost = pl.CostEstimate(
        flops=2 * rows * tiles * bs * bs * width,
        bytes_accessed=2 * rows * tiles * bs * bs + 2 * blocks.size + 2 * rows * bs * width,
        transcendentals=0,
    )
    out = pl.pallas_call(
        _product_kernel,
        grid_spec=pltpu.PrefetchScalarGridSpec(
            num_scalar_prefetch=1,
            grid=(rows // group,),
            in_specs=[
                pl.BlockSpec((group, tiles, bs, bs), lambda p, pos: (p, 0, 0, 0)),
                pl.BlockSpec(blocks.shape, lambda p, pos: (0, 0, 0), pipeline_mode=pl.Buffered(1)),
            ],
            out_specs=pl.BlockSpec((group, bs, width), lambda p, pos: (p, 0, 0)),
        ),
        out_shape=jax.ShapeDtypeStruct((rows, bs, width), jnp.bfloat16),
        compiler_params=pltpu.CompilerParams(
            dimension_semantics=("arbitrary",), vmem_limit_bytes=48 * 1024 * 1024
        ),
        cost_estimate=cost,
    )(positions.reshape(-1), adjacency_tiles, blocks)
    return out.reshape(rows * bs, width)


def xor_pairs(size, bit):
    return [(i, i ^ bit) for i in range(size)]


def butterfly_sum(x, axis, size):
    bit = 1
    while bit < size:
        x = x + lax.ppermute(x, axis, xor_pairs(size, bit))
        bit *= 2
    return x


def halving_scatter(parts, axis, size):
    me = lax.axis_index(axis)
    bit = size // 2
    while bit >= 1:
        half = parts.shape[0] // 2
        lo, hi = parts[:half], parts[half:]
        mine_hi = (me & bit) != 0
        keep = jnp.where(mine_hi, hi, lo)
        send = jnp.where(mine_hi, lo, hi)
        parts = keep + lax.ppermute(send, axis, xor_pairs(size, bit))
        bit //= 2
    return parts[0]


def doubling_gather(x, axis, size):
    me = lax.axis_index(axis)
    bit = 1
    while bit < size:
        got = lax.ppermute(x, axis, xor_pairs(size, bit))
        x = jnp.where((me & bit) != 0, jnp.concatenate([got, x]), jnp.concatenate([x, got]))
        bit *= 2
    return x


BLK = ("z", "xh", "y")
REP = ("xl", "c")


def exchange(parts, size, far=False, ordered=True):
    me = lax.axis_index(REP)
    axis = ("xh",) + REP if far else REP
    got = []
    for s in range(size):
        send = lax.dynamic_index_in_dim(parts, me ^ s, 0, keepdims=False)
        if far:
            send = lax.ppermute(send, axis, xor_pairs(2 * size, size + s))
        elif s:
            send = lax.ppermute(send, axis, xor_pairs(size, s))
        got.append(send)
    got = jnp.stack(got)
    return jnp.take(got, jnp.arange(size) ^ me, axis=0) if ordered else got


def hier_gather(x):
    pieces = jnp.split(x, 4, axis=0)
    partner = [lax.ppermute(piece, "xh", xor_pairs(2, 1)) for piece in pieces]
    pair = jnp.concatenate([x] + partner, axis=0)
    return lax.all_gather(pair, ("y", "z"), axis=0, tiled=True)


def hier_positions(positions, local_blocks, n_z, n_xh, n_y, piece_blocks=None):
    owner, block = positions // local_blocks, positions % local_blocks
    if piece_blocks:
        piece = (block // piece_blocks) ^ lax.axis_index(REP)
        block = piece * piece_blocks + block % piece_blocks
    z, xh, y = owner // (n_xh * n_y), (owner // n_y) % n_xh, owner % n_y
    slot = xh ^ lax.axis_index("xh")
    return ((y * n_z + z) * n_xh + slot) * local_blocks + block


def local(sizes, node_features, weight, cotangent, adjacency_tiles, block_cols, block_perm):
    n_z, n_xh, n_y, n_xl, n_c = sizes
    n_blk, n_rep = n_z * n_xh * n_y, n_xl * n_c
    feat_dev = node_features.shape[1]
    f_all = weight.shape[0]
    bs = adjacency_tiles.shape[2]
    w_split = weight.reshape(n_rep, feat_dev, f_all)
    positions = column_positions(block_cols, block_perm)
    raw, lb = positions, node_features.shape[0] // bs
    positions = hier_positions(raw, lb, n_z, n_xh, n_y)
    gathered = hier_gather(node_features)
    aggregate = block_product(adjacency_tiles, positions, gathered)
    rows = aggregate.shape[0] // n_rep
    flip = jnp.arange(n_rep) ^ lax.axis_index(REP)
    agg_got = exchange(aggregate.reshape(n_rep, rows, feat_dev), n_rep, ordered=False)
    w_got = jnp.take(w_split, flip, axis=0)
    preact = jnp.einsum("irf,ifo->ro", agg_got, w_got, preferred_element_type=jnp.float32)
    gating = jax.nn.sigmoid(preact)
    activated = (preact * gating).astype(jnp.bfloat16)
    slopes = gating * (1.0 + preact * (1.0 - gating))
    grad_pre = (cotangent.astype(jnp.float32) * slopes).astype(jnp.bfloat16)
    grad_split = jnp.einsum(
        "rf,jof->jro", grad_pre, w_split, preferred_element_type=jnp.float32
    ).astype(jnp.bfloat16)
    own = exchange(grad_split, n_rep, ordered=False)
    far = exchange(grad_split, n_rep, far=True, ordered=False)
    pair = jnp.concatenate([own, far])
    gathered_grad = lax.all_gather(pair.reshape(-1, feat_dev), ("y", "z"), axis=0, tiled=True)
    grad_positions = hier_positions(raw, lb, n_z, n_xh, n_y, rows // bs)
    feature_grad = block_product(adjacency_tiles, grad_positions, gathered_grad)
    agg_rows = jnp.take(agg_got, flip, axis=0)
    weight_part = jnp.einsum("irf,ro->ifo", agg_rows, grad_pre, preferred_element_type=jnp.float32)
    weight_rows = halving_scatter(weight_part, REP, n_rep)
    node_total = node_features.shape[0] * n_blk
    quarter = halving_scatter(weight_rows.reshape(n_y, -1, f_all), "y", n_y)
    quarter = butterfly_sum(quarter, ("z", "xh"), n_z * n_xh)
    weight_grad = doubling_gather(quarter, "y", n_y) * (1.0 / math.sqrt(node_total))
    return (activated, feature_grad, weight_grad)


def solution(mesh):
    n_blk, n_rep = mesh.shape["blk"], mesh.shape["rep"]
    sizes = (n_blk // 8, 2, 4, n_rep // 2, 2)
    fine = Mesh(mesh.devices.reshape(sizes), BLK + REP)
    return jax.shard_map(
        functools.partial(local, sizes),
        mesh=fine,
        in_specs=(
            P(BLK, REP),
            P(),
            P(BLK + REP, None),
            P(BLK, None, None, None),
            P(BLK, None),
            P(),
        ),
        out_specs=(P(BLK + REP, None), P(BLK, REP), P(REP, None)),
        check_vma=False,
    )
```

```python
import functools
import math

import jax
import jax.numpy as jnp
from jax import lax
from jax.experimental import pallas as pl
from jax.experimental.pallas import tpu as pltpu
from jax.sharding import Mesh, PartitionSpec as P


def column_positions(block_cols, block_perm):
    numbers = jnp.arange(block_perm.shape[0], dtype=jnp.int32)
    matches = block_cols[:, :, None] == numbers[None, None, :]
    return jnp.sum(jnp.where(matches, block_perm[None, None, :], 0), axis=-1)


def _product_kernel(pos_ref, a_ref, x_ref, o_ref):
    step = pl.program_id(0)
    group, tiles = a_ref.shape[0], a_ref.shape[1]
    for g in range(group):
        base = (step * group + g) * tiles
        lhs = jnp.concatenate([a_ref[g, k] for k in range(tiles)], axis=1)
        rhs = jnp.concatenate([x_ref[pos_ref[base + k]] for k in range(tiles)], axis=0)
        o_ref[g] = jnp.dot(lhs, rhs, preferred_element_type=jnp.float32).astype(o_ref.dtype)


def block_product(adjacency_tiles, positions, gathered):
    rows, tiles, bs, _ = adjacency_tiles.shape
    width = gathered.shape[1]
    group = 4 if rows % 4 == 0 else 1
    blocks = gathered.reshape(-1, bs, width)
    cost = pl.CostEstimate(
        flops=2 * rows * tiles * bs * bs * width,
        bytes_accessed=2 * rows * tiles * bs * bs + 2 * blocks.size + 2 * rows * bs * width,
        transcendentals=0,
    )
    out = pl.pallas_call(
        _product_kernel,
        grid_spec=pltpu.PrefetchScalarGridSpec(
            num_scalar_prefetch=1,
            grid=(rows // group,),
            in_specs=[
                pl.BlockSpec((group, tiles, bs, bs), lambda p, pos: (p, 0, 0, 0)),
                pl.BlockSpec(blocks.shape, lambda p, pos: (0, 0, 0), pipeline_mode=pl.Buffered(1)),
            ],
            out_specs=pl.BlockSpec((group, bs, width), lambda p, pos: (p, 0, 0)),
        ),
        out_shape=jax.ShapeDtypeStruct((rows, bs, width), jnp.bfloat16),
        compiler_params=pltpu.CompilerParams(
            dimension_semantics=("arbitrary",), vmem_limit_bytes=48 * 1024 * 1024
        ),
        cost_estimate=cost,
    )(positions.reshape(-1), adjacency_tiles, blocks)
    return out.reshape(rows * bs, width)


def xor_pairs(size, bit):
    return [(i, i ^ bit) for i in range(size)]


def butterfly_sum(x, axis, size):
    bit = 1
    while bit < size:
        x = x + lax.ppermute(x, axis, xor_pairs(size, bit))
        bit *= 2
    return x


def halving_scatter(parts, axis, size):
    me = lax.axis_index(axis)
    bit = size // 2
    while bit >= 1:
        half = parts.shape[0] // 2
        lo, hi = parts[:half], parts[half:]
        mine_hi = (me & bit) != 0
        keep = jnp.where(mine_hi, hi, lo)
        send = jnp.where(mine_hi, lo, hi)
        parts = keep + lax.ppermute(send, axis, xor_pairs(size, bit))
        bit //= 2
    return parts[0]


def doubling_gather(x, axis, size):
    me = lax.axis_index(axis)
    bit = 1
    while bit < size:
        got = lax.ppermute(x, axis, xor_pairs(size, bit))
        x = jnp.where((me & bit) != 0, jnp.concatenate([got, x]), jnp.concatenate([x, got]))
        bit *= 2
    return x


BLK = ("z", "xh", "y")
REP = ("xl", "c")


def exchange(parts, size, far=False, ordered=True):
    me = lax.axis_index(REP)
    axis = ("xh",) + REP if far else REP
    got = []
    for s in range(size):
        send = lax.dynamic_index_in_dim(parts, me ^ s, 0, keepdims=False)
        if far:
            send = lax.ppermute(send, axis, xor_pairs(2 * size, size + s))
        elif s:
            send = lax.ppermute(send, axis, xor_pairs(size, s))
        got.append(send)
    got = jnp.stack(got)
    return jnp.take(got, jnp.arange(size) ^ me, axis=0) if ordered else got


def hier_gather(x):
    partner = lax.ppermute(x, "xh", xor_pairs(2, 1))
    pair = jnp.concatenate([x, partner], axis=0)
    return lax.all_gather(pair, ("y", "z"), axis=0, tiled=True)


def hier_positions(positions, local_blocks, n_z, n_xh, n_y, piece_blocks=None):
    owner, block = positions // local_blocks, positions % local_blocks
    if piece_blocks:
        piece = (block // piece_blocks) ^ lax.axis_index(REP)
        block = piece * piece_blocks + block % piece_blocks
    z, xh, y = owner // (n_xh * n_y), (owner // n_y) % n_xh, owner % n_y
    slot = xh ^ lax.axis_index("xh")
    return ((y * n_z + z) * n_xh + slot) * local_blocks + block


def local(sizes, node_features, weight, cotangent, adjacency_tiles, block_cols, block_perm):
    n_z, n_xh, n_y, n_xl, n_c = sizes
    n_blk, n_rep = n_z * n_xh * n_y, n_xl * n_c
    feat_dev = node_features.shape[1]
    f_all = weight.shape[0]
    bs = adjacency_tiles.shape[2]
    w_split = weight.reshape(n_rep, feat_dev, f_all)
    positions = column_positions(block_cols, block_perm)
    raw, lb = positions, node_features.shape[0] // bs
    positions = hier_positions(raw, lb, n_z, n_xh, n_y)
    gathered = hier_gather(node_features)
    aggregate = block_product(adjacency_tiles, positions, gathered)
    rows = aggregate.shape[0] // n_rep
    flip = jnp.arange(n_rep) ^ lax.axis_index(REP)
    agg_got = exchange(aggregate.reshape(n_rep, rows, feat_dev), n_rep, ordered=False)
    w_got = jnp.take(w_split, flip, axis=0)
    preact = jnp.einsum("irf,ifo->ro", agg_got, w_got, preferred_element_type=jnp.float32)
    gating = jax.nn.sigmoid(preact)
    activated = (preact * gating).astype(jnp.bfloat16)
    slopes = gating * (1.0 + preact * (1.0 - gating))
    grad_pre = (cotangent.astype(jnp.float32) * slopes).astype(jnp.bfloat16)
    grad_split = jnp.einsum(
        "rf,jof->jro", grad_pre, w_split, preferred_element_type=jnp.float32
    ).astype(jnp.bfloat16)
    own = exchange(grad_split, n_rep, ordered=False)
    far = exchange(grad_split, n_rep, far=True, ordered=False)
    pair = jnp.concatenate([own, far])
    gathered_grad = lax.all_gather(pair.reshape(-1, feat_dev), ("y", "z"), axis=0, tiled=True)
    grad_positions = hier_positions(raw, lb, n_z, n_xh, n_y, rows // bs)
    feature_grad = block_product(adjacency_tiles, grad_positions, gathered_grad)
    agg_rows = jnp.take(agg_got, flip, axis=0)
    weight_part = jnp.einsum("irf,ro->ifo", agg_rows, grad_pre, preferred_element_type=jnp.float32)
    weight_rows = halving_scatter(weight_part, REP, n_rep)
    node_total = node_features.shape[0] * n_blk
    quarter = halving_scatter(weight_rows.reshape(n_y, -1, f_all), "y", n_y)
    quarter = butterfly_sum(quarter, ("z", "xh"), n_z * n_xh)
    weight_grad = doubling_gather(quarter, "y", n_y) * (1.0 / math.sqrt(node_total))
    return (activated, feature_grad, weight_grad)


def solution(mesh):
    n_blk, n_rep = mesh.shape["blk"], mesh.shape["rep"]
    sizes = (n_blk // 8, 2, 4, n_rep // 2, 2)
    fine = Mesh(mesh.devices.reshape(sizes), BLK + REP)
    return jax.shard_map(
        functools.partial(local, sizes),
        mesh=fine,
        in_specs=(
            P(BLK, REP),
            P(),
            P(BLK + REP, None),
            P(BLK, None, None, None),
            P(BLK, None),
            P(),
        ),
        out_specs=(P(BLK + REP, None), P(BLK, REP), P(REP, None)),
        check_vma=False,
    )
```

```python
import functools
import math

import jax
import jax.numpy as jnp
from jax import lax
from jax.experimental import pallas as pl
from jax.experimental.pallas import tpu as pltpu
from jax.sharding import Mesh, PartitionSpec as P


def column_positions(block_cols, block_perm):
    numbers = jnp.arange(block_perm.shape[0], dtype=jnp.int32)
    matches = block_cols[:, :, None] == numbers[None, None, :]
    return jnp.sum(jnp.where(matches, block_perm[None, None, :], 0), axis=-1)


def _product_kernel(pos_ref, a_ref, x_ref, o_ref):
    step = pl.program_id(0)
    group, tiles = a_ref.shape[0], a_ref.shape[1]
    for g in range(group):
        base = (step * group + g) * tiles
        lhs = jnp.concatenate([a_ref[g, k] for k in range(tiles)], axis=1)
        rhs = jnp.concatenate([x_ref[pos_ref[base + k]] for k in range(tiles)], axis=0)
        o_ref[g] = jnp.dot(lhs, rhs, preferred_element_type=jnp.float32).astype(o_ref.dtype)


def block_product(adjacency_tiles, positions, gathered):
    rows, tiles, bs, _ = adjacency_tiles.shape
    width = gathered.shape[1]
    group = 6 if rows % 6 == 0 else 1
    blocks = gathered.reshape(-1, bs, width)
    cost = pl.CostEstimate(
        flops=2 * rows * tiles * bs * bs * width,
        bytes_accessed=2 * rows * tiles * bs * bs + 2 * blocks.size + 2 * rows * bs * width,
        transcendentals=0,
    )
    out = pl.pallas_call(
        _product_kernel,
        grid_spec=pltpu.PrefetchScalarGridSpec(
            num_scalar_prefetch=1,
            grid=(rows // group,),
            in_specs=[
                pl.BlockSpec((group, tiles, bs, bs), lambda p, pos: (p, 0, 0, 0)),
                pl.BlockSpec(blocks.shape, lambda p, pos: (0, 0, 0), pipeline_mode=pl.Buffered(1)),
            ],
            out_specs=pl.BlockSpec((group, bs, width), lambda p, pos: (p, 0, 0)),
        ),
        out_shape=jax.ShapeDtypeStruct((rows, bs, width), jnp.bfloat16),
        compiler_params=pltpu.CompilerParams(
            dimension_semantics=("arbitrary",), vmem_limit_bytes=48 * 1024 * 1024
        ),
        cost_estimate=cost,
    )(positions.reshape(-1), adjacency_tiles, blocks)
    return out.reshape(rows * bs, width)


def xor_pairs(size, bit):
    return [(i, i ^ bit) for i in range(size)]


def butterfly_sum(x, axis, size):
    bit = 1
    while bit < size:
        x = x + lax.ppermute(x, axis, xor_pairs(size, bit))
        bit *= 2
    return x


def halving_scatter(parts, axis, size):
    me = lax.axis_index(axis)
    bit = size // 2
    while bit >= 1:
        half = parts.shape[0] // 2
        lo, hi = parts[:half], parts[half:]
        mine_hi = (me & bit) != 0
        keep = jnp.where(mine_hi, hi, lo)
        send = jnp.where(mine_hi, lo, hi)
        parts = keep + lax.ppermute(send, axis, xor_pairs(size, bit))
        bit //= 2
    return parts[0]


def doubling_gather(x, axis, size):
    me = lax.axis_index(axis)
    bit = 1
    while bit < size:
        got = lax.ppermute(x, axis, xor_pairs(size, bit))
        x = jnp.where((me & bit) != 0, jnp.concatenate([got, x]), jnp.concatenate([x, got]))
        bit *= 2
    return x


BLK = ("z", "xh", "y")
REP = ("xl", "c")


def exchange(parts, size, far=False, ordered=True):
    me = lax.axis_index(REP)
    axis = ("xh",) + REP if far else REP
    got = []
    for s in range(size):
        send = lax.dynamic_index_in_dim(parts, me ^ s, 0, keepdims=False)
        if far:
            send = lax.ppermute(send, axis, xor_pairs(2 * size, size + s))
        elif s:
            send = lax.ppermute(send, axis, xor_pairs(size, s))
        got.append(send)
    got = jnp.stack(got)
    return jnp.take(got, jnp.arange(size) ^ me, axis=0) if ordered else got


def hier_gather(x):
    partner = lax.ppermute(x, "xh", xor_pairs(2, 1))
    pair = jnp.concatenate([x, partner], axis=0)
    return lax.all_gather(pair, ("y", "z"), axis=0, tiled=True)


def hier_positions(positions, local_blocks, n_z, n_xh, n_y, piece_blocks=None):
    owner, block = positions // local_blocks, positions % local_blocks
    if piece_blocks:
        piece = (block // piece_blocks) ^ lax.axis_index(REP)
        block = piece * piece_blocks + block % piece_blocks
    z, xh, y = owner // (n_xh * n_y), (owner // n_y) % n_xh, owner % n_y
    slot = xh ^ lax.axis_index("xh")
    return ((y * n_z + z) * n_xh + slot) * local_blocks + block


def local(sizes, node_features, weight, cotangent, adjacency_tiles, block_cols, block_perm):
    n_z, n_xh, n_y, n_xl, n_c = sizes
    n_blk, n_rep = n_z * n_xh * n_y, n_xl * n_c
    feat_dev = node_features.shape[1]
    f_all = weight.shape[0]
    bs = adjacency_tiles.shape[2]
    w_split = weight.reshape(n_rep, feat_dev, f_all)
    positions = column_positions(block_cols, block_perm)
    raw, lb = positions, node_features.shape[0] // bs
    positions = hier_positions(raw, lb, n_z, n_xh, n_y)
    gathered = hier_gather(node_features)
    aggregate = block_product(adjacency_tiles, positions, gathered)
    rows = aggregate.shape[0] // n_rep
    flip = jnp.arange(n_rep) ^ lax.axis_index(REP)
    agg_got = exchange(aggregate.reshape(n_rep, rows, feat_dev), n_rep, ordered=False)
    w_got = jnp.take(w_split, flip, axis=0)
    preact = jnp.einsum("irf,ifo->ro", agg_got, w_got, preferred_element_type=jnp.float32)
    gating = jax.nn.sigmoid(preact)
    activated = (preact * gating).astype(jnp.bfloat16)
    slopes = gating * (1.0 + preact * (1.0 - gating))
    grad_pre = (cotangent.astype(jnp.float32) * slopes).astype(jnp.bfloat16)
    grad_split = jnp.einsum(
        "rf,jof->jro", grad_pre, w_split, preferred_element_type=jnp.float32
    ).astype(jnp.bfloat16)
    own = exchange(grad_split, n_rep, ordered=False)
    far = exchange(grad_split, n_rep, far=True, ordered=False)
    pair = jnp.concatenate([own, far])
    gathered_grad = lax.all_gather(pair.reshape(-1, feat_dev), ("y", "z"), axis=0, tiled=True)
    grad_positions = hier_positions(raw, lb, n_z, n_xh, n_y, rows // bs)
    feature_grad = block_product(adjacency_tiles, grad_positions, gathered_grad)
    agg_rows = jnp.take(agg_got, flip, axis=0)
    weight_part = jnp.einsum("irf,ro->ifo", agg_rows, grad_pre, preferred_element_type=jnp.float32)
    weight_rows = halving_scatter(weight_part, REP, n_rep)
    node_total = node_features.shape[0] * n_blk
    quarter = halving_scatter(weight_rows.reshape(n_y, -1, f_all), "y", n_y)
    quarter = butterfly_sum(quarter, ("z", "xh"), n_z * n_xh)
    weight_grad = doubling_gather(quarter, "y", n_y) * (1.0 / math.sqrt(node_total))
    return (activated, feature_grad, weight_grad)


def solution(mesh):
    n_blk, n_rep = mesh.shape["blk"], mesh.shape["rep"]
    sizes = (n_blk // 8, 2, 4, n_rep // 2, 2)
    fine = Mesh(mesh.devices.reshape(sizes), BLK + REP)
    return jax.shard_map(
        functools.partial(local, sizes),
        mesh=fine,
        in_specs=(
            P(BLK, REP),
            P(),
            P(BLK + REP, None),
            P(BLK, None, None, None),
            P(BLK, None),
            P(),
        ),
        out_specs=(P(BLK + REP, None), P(BLK, REP), P(REP, None)),
        check_vma=False,
    )
```
